128 devices in a mesh: dp: 8 (over z, core), seq: 16 (over y, x).
Axes of the slice: x: 4, y: 4, z: 4, core: 2. Of those that a mesh axis runs over, the one named last changes fastest.
Arguments:
- tokens: bfloat16 [8, 8192, 2048], P('dp', 'seq'), may hold values from -6 to 6
- input_gain: bfloat16 [2048], replicated, may hold values from 0.099609375 to 1.8984375
- qkv_weight: bfloat16 [2048, 6144], P(None, ('dp', 'seq')), may hold values from -0.125 to 0.125
- head_gain: bfloat16 [2048], replicated, may hold values from 0.099609375 to 1.8984375
- prefix_state: float32 [8, 16, 128, 128], P('dp'), may hold values from -256 to 256
Outputs:
- attended: bfloat16 [8, 8192, 2048], P('dp', 'seq')
The draws below stay inside these ranges and needn't reach their ends.
All inputs are finite; a program needn't handle non-finite values.
Results may differ from the reference program's by a relative error of at most 0.0061.
Values may be sent and summed in bfloat16 or wider, within the bound.
No kernel may reach another device: no remote copies, remote signals or barrier semaphores. Data moves between devices by JAX's collectives and lax.ppermute only.
A program may use at most 128 MiB of HBM per device.

```python
import jax
import jax.numpy as jnp
from jax import lax

D = 2048
H = 16
DH = 128
TOK_DEV = 512
BLOCK = 512
LENGTH = 8192
SEQS = 8
N_SEQ = 16


def level_of(rng, shape, cuts, least, high):
    loudness, own = 1.0, jax.random.fold_in(rng, 6)
    for position, parts in cuts:
        heights = jnp.exp(jax.random.uniform(jax.random.fold_in(own, position), (parts,), jnp.float32, least / len(cuts), high / len(cuts)))
        loudness = loudness * jnp.repeat(heights, shape[position] // parts).reshape([-1 if axis == position else 1 for axis in range(len(shape))])
    return loudness


def gaussian(key, dims, deviation, bound, cuts=(), held_as=jnp.bfloat16):
    level = level_of(key, dims, cuts, -0.22, 0.18) if cuts else 1.0
    array = jax.random.normal(key, dims, jnp.float32) * deviation * level
    return jnp.minimum(jnp.maximum(array, -bound), bound).astype(held_as)


def setup_inputs(seed: int = 0) -> dict:
    arg_keys = jax.random.split(jax.random.key(seed), 6)
    tokens = gaussian(arg_keys[0], (SEQS, LENGTH, D), 1.0, 6.0, ((0, 8), (1, 16)))
    input_gain = jnp.clip(1.0 + 0.18 * jax.random.normal(arg_keys[1], (D,), jnp.float32), 0.099609375, 1.8984375).astype(jnp.bfloat16)
    qkv_weight = gaussian(arg_keys[2], (D, 3 * D), D ** -0.5, 0.125, ((1, 128),))
    head_gain = jnp.clip(1.0 + 0.18 * jax.random.normal(arg_keys[3], (D,), jnp.float32), 0.099609375, 1.8984375).astype(jnp.bfloat16)
    prefix_state = gaussian(arg_keys[4], (SEQS, H, DH, DH), (2 * TOK_DEV ** 0.5), 256.0, ((0, 8),), jnp.float32)
    return dict(tokens=tokens, input_gain=input_gain, qkv_weight=qkv_weight, head_gain=head_gain, prefix_state=prefix_state)


epsilon = 1e-05

def feature_map(inputs):
    return jnp.where(inputs > 0, inputs + 1.0, jnp.exp(jnp.minimum(inputs, 0.0)))

def rounded(inputs):
    return lax.optimization_barrier(inputs.astype(jnp.bfloat16)).astype(jnp.float32)

def span_attention(queries, key_feats, values, memory, head_gain):
    num_blocks = queries.shape[0] // BLOCK
    causal = jnp.arange(BLOCK)[:, None] >= jnp.arange(BLOCK)[None, :]
    gains = head_gain.astype(jnp.float32).reshape(H, DH)

    def advance(running, blocks):
        query_blk, key_blk, value_blk = blocks
        carried = jnp.einsum('bhd,hde->bhe', query_blk, rounded(running))
        scores = jnp.einsum('bhd,chd->hbc', query_blk, key_blk)
        scores = jnp.where(causal[None], scores, 0.0)
        within = jnp.einsum('hbc,che->bhe', rounded(scores), value_blk)
        numerator = carried + within
        scale = lax.rsqrt(lax.optimization_barrier(jnp.mean(numerator * numerator, axis=-1, keepdims=True)) + epsilon)
        running = running + jnp.einsum('bhd,bhe->hde', key_blk, value_blk)
        return (running, (numerator * scale * gains).astype(jnp.bfloat16))

    def shaped(inputs):
        return inputs.astype(jnp.float32).reshape(num_blocks, BLOCK, H, DH)
    final_memory, outputs = lax.scan(advance, memory, (shaped(queries), shaped(key_feats), shaped(values)))
    return outputs.reshape(num_blocks * BLOCK, H * DH)

def reference(tokens, input_gain, qkv_weight, head_gain, prefix_state):

    def one_sequence(group):
        seq_tokens, seq_prefix = group
        inputs = seq_tokens.astype(jnp.float32)
        normed = inputs * lax.rsqrt(lax.optimization_barrier(jnp.mean(inputs * inputs, axis=-1, keepdims=True)) + epsilon)
        normed = (normed * input_gain.astype(jnp.float32)).astype(jnp.bfloat16)
        projected = jnp.dot(normed, qkv_weight, preferred_element_type=jnp.float32)
        queries = feature_map(projected[:, :D]).astype(jnp.bfloat16).reshape(N_SEQ, TOK_DEV, H, DH)
        key_feats = feature_map(projected[:, D:2 * D]).astype(jnp.bfloat16).reshape(N_SEQ, TOK_DEV, H, DH)
        values = projected[:, 2 * D:].astype(jnp.bfloat16).reshape(N_SEQ, TOK_DEV, H, DH)
        local = rounded(jnp.einsum('cthd,cthe->chde', key_feats.astype(jnp.float32), values.astype(jnp.float32)))
        totals = jnp.cumsum(local, axis=0)
        before = jnp.concatenate([jnp.zeros((1, H, DH, DH), jnp.float32), totals[:-1]], axis=0)
        memory = seq_prefix[None] + before

        def one_piece(pieces):
            return span_attention(pieces[0], pieces[1], pieces[2], pieces[3], head_gain)
        attended = lax.map(one_piece, (queries, key_feats, values, memory))
        return attended.reshape(LENGTH, D)
    return lax.map(one_sequence, (tokens, prefix_state))
```

```python
import jax
import jax.numpy as jnp
from jax import lax
from jax.sharding import Mesh, PartitionSpec as P

D = 2048
H = 16
DH = 128
BLOCK = 512


epsilon = 1e-05


def feature_map(inputs):
    return jnp.where(inputs > 0, inputs + 1.0, jnp.exp(jnp.minimum(inputs, 0.0)))


def span_attention(queries, key_feats, values, memory, head_gain):
    num_blocks = queries.shape[0] // BLOCK
    causal = jnp.arange(BLOCK)[:, None] >= jnp.arange(BLOCK)[None, :]
    gains = head_gain.astype(jnp.float32).reshape(H, DH)

    def advance(running, blocks):
        query_blk, key_blk, value_blk = blocks
        carried = jnp.einsum(
            "bhd,hde->bhe",
            query_blk,
            running.astype(jnp.bfloat16),
            preferred_element_type=jnp.float32,
        )
        scores = jnp.einsum("bhd,chd->hbc", query_blk, key_blk, preferred_element_type=jnp.float32)
        scores = jnp.where(causal[None], scores, 0.0).astype(jnp.bfloat16)
        within = jnp.einsum("hbc,che->bhe", scores, value_blk, preferred_element_type=jnp.float32)
        numerator = carried + within
        scale = lax.rsqrt(jnp.mean(numerator * numerator, axis=-1, keepdims=True) + epsilon)
        running = running + jnp.einsum(
            "bhd,bhe->hde", key_blk, value_blk, preferred_element_type=jnp.float32
        )
        return (running, (numerator * scale * gains).astype(jnp.bfloat16))

    def shaped(inputs):
        return inputs.reshape(num_blocks, BLOCK, H, DH)

    final_memory, outputs = lax.scan(
        advance, memory, (shaped(queries), shaped(key_feats), shaped(values))
    )
    return outputs.reshape(num_blocks * BLOCK, H * DH)


def body(tokens, input_gain, qkv_weight, head_gain, prefix_state):
    swap = [(0, 1), (1, 0)]
    core = lax.axis_index("c")
    inputs = tokens[0].astype(jnp.float32)
    normed = inputs * lax.rsqrt(jnp.mean(inputs * inputs, axis=-1, keepdims=True) + epsilon)
    normed = (normed * input_gain.astype(jnp.float32)).astype(jnp.bfloat16)
    tok_rows = normed.shape[0]
    partner = lax.ppermute(normed, "c", swap)
    both = jnp.concatenate([normed, partner], axis=0)
    half_w = lax.all_gather(qkv_weight, ("z", "seq"), axis=1, tiled=True)
    n_z = half_w.shape[1] // qkv_weight.shape[1] // lax.axis_size("seq")
    span = half_w.shape[1] // n_z
    projected = jnp.dot(both, half_w, preferred_element_type=jnp.float32)
    col = jnp.arange(half_w.shape[1])
    global_col = (2 * (col // span) + core) * span + col % span
    feats = jnp.where(global_col < 2 * D, feature_map(projected), projected).astype(jnp.bfloat16)
    mine = feats[:tok_rows].reshape(tok_rows, n_z, 1, span)
    theirs = lax.ppermute(feats[tok_rows:], "c", swap).reshape(tok_rows, n_z, 1, span)
    full = jnp.where(
        core == 0,
        jnp.concatenate([mine, theirs], axis=2),
        jnp.concatenate([theirs, mine], axis=2),
    ).reshape(tok_rows, 3 * D)
    queries = full[:, :D].reshape(tok_rows, H, DH)
    key_feats = full[:, D : 2 * D].reshape(tok_rows, H, DH)
    values = full[:, 2 * D :].reshape(tok_rows, H, DH)
    local = jnp.einsum(
        "thd,the->hde", key_feats, values, preferred_element_type=jnp.float32
    ).astype(jnp.bfloat16)
    gathered = lax.all_gather(local[None], "seq", axis=0, tiled=True)
    my_index = lax.axis_index("seq")
    earlier = (jnp.arange(gathered.shape[0]) < my_index).astype(jnp.bfloat16)
    before = jnp.einsum("c,chde->hde", earlier, gathered, preferred_element_type=jnp.float32)
    memory = prefix_state[0] + before
    attended = span_attention(queries, key_feats, values, memory, head_gain)
    return attended[None]


def solution(mesh):
    n_dp, n_seq = mesh.devices.shape
    split = Mesh(mesh.devices.reshape(n_dp // 2, 2, n_seq), ("z", "c", "seq"))
    rows = ("z", "c")
    placed = (P(rows, "seq", None), P(), P(None, ("z", "c", "seq")), P(), P(rows, None, None, None))
    return jax.shard_map(
        body, mesh=split, in_specs=placed, out_specs=P(rows, "seq", None), check_vma=False
    )
```

```python
import jax
import jax.numpy as jnp
from jax import lax
from jax.sharding import Mesh, PartitionSpec as P

D = 2048
H = 16
DH = 128
BLOCK = 512


epsilon = 1e-05


def feature_map(inputs):
    return jnp.where(inputs > 0, inputs + 1.0, jnp.exp(jnp.minimum(inputs, 0.0)))


def span_attention(queries, key_feats, values, memory, head_gain):
    num_blocks = queries.shape[0] // BLOCK
    causal = jnp.arange(BLOCK)[:, None] >= jnp.arange(BLOCK)[None, :]
    gains = head_gain.astype(jnp.float32).reshape(H, DH)

    def advance(running, blocks):
        query_blk, key_blk, value_blk = blocks
        carried = jnp.einsum(
            "bhd,hde->bhe",
            query_blk,
            running.astype(jnp.bfloat16),
            preferred_element_type=jnp.float32,
        )
        scores = jnp.einsum("bhd,chd->hbc", query_blk, key_blk, preferred_element_type=jnp.float32)
        scores = jnp.where(causal[None], scores, 0.0).astype(jnp.bfloat16)
        within = jnp.einsum("hbc,che->bhe", scores, value_blk, preferred_element_type=jnp.float32)
        numerator = carried + within
        scale = lax.rsqrt(jnp.mean(numerator * numerator, axis=-1, keepdims=True) + epsilon)
        running = running + jnp.einsum(
            "bhd,bhe->hde", key_blk, value_blk, preferred_element_type=jnp.float32
        )
        return (running, (numerator * scale * gains).astype(jnp.bfloat16))

    def shaped(inputs):
        return inputs.reshape(num_blocks, BLOCK, H, DH)

    final_memory, outputs = lax.scan(
        advance, memory, (shaped(queries), shaped(key_feats), shaped(values))
    )
    return outputs.reshape(num_blocks * BLOCK, H * DH)


def ring_gather(value, axis, size):
    here = lax.axis_index(axis)
    out = jnp.zeros((size,) + value.shape, value.dtype)
    out = lax.dynamic_update_index_in_dim(out, value, here, 0)
    for shift in range(1, size):
        got = lax.ppermute(value, axis, [(j, (j + shift) % size) for j in range(size)])
        out = lax.dynamic_update_index_in_dim(out, got, (here - shift) % size, 0)
    return out


def gather_half_weight(qkv_weight):
    wt = qkv_weight.T
    n_part = 3
    width = wt.shape[0] // n_part
    orders = (("x", "y", "z"), ("y", "z", "x"), ("z", "x", "y"))
    parts = []
    for p in range(n_part):
        piece = wt[p * width : (p + 1) * width]
        for axis in orders[p]:
            piece = ring_gather(piece, axis, lax.axis_size(axis))
        parts.append(piece)
    return parts, orders


def body(tokens, input_gain, qkv_weight, head_gain, prefix_state):
    swap = [(0, 1), (1, 0)]
    core = lax.axis_index("c")
    inputs = tokens[0].astype(jnp.float32)
    normed = inputs * lax.rsqrt(jnp.mean(inputs * inputs, axis=-1, keepdims=True) + epsilon)
    normed = (normed * input_gain.astype(jnp.float32)).astype(jnp.bfloat16)
    tok_rows = normed.shape[0]
    partner = lax.ppermute(normed, "c", swap)
    both = jnp.concatenate([normed, partner], axis=0)
    parts, orders = gather_half_weight(qkv_weight)
    n_c = 2
    sizes = {a: lax.axis_size(a) for a in ("z", "y", "x")}
    width = parts[0].shape[-2]
    per_dev = width * len(parts)
    mine, theirs = [], []
    for p, wpart in enumerate(parts):
        names = orders[p][::-1]
        dims = [sizes[a] for a in names]
        proj = jnp.dot(both, wpart.reshape(-1, wpart.shape[-1]).T, preferred_element_type=jnp.float32)
        proj = proj.reshape([2 * tok_rows] + dims + [width])
        coord = {}
        for k, a in enumerate(names):
            shape = [1] * 5
            shape[k + 1] = dims[k]
            coord[a] = jnp.arange(dims[k]).reshape(shape)
        dev = ((coord["z"] * n_c + core) * sizes["y"] + coord["y"]) * sizes["x"] + coord["x"]
        global_col = dev * per_dev + p * width + jnp.arange(width).reshape(1, 1, 1, 1, width)
        feats = jnp.where(global_col < 2 * D, feature_map(proj), proj).astype(jnp.bfloat16)
        back = [0] + [1 + names.index(a) for a in ("z", "y", "x")] + [4]
        mine.append(jnp.transpose(feats[:tok_rows], back))
        theirs.append(jnp.transpose(lax.ppermute(feats[tok_rows:], "c", swap), back))
    mine = jnp.stack(mine, axis=-2)
    theirs = jnp.stack(theirs, axis=-2)
    full = jnp.where(
        core == 0,
        jnp.stack([mine, theirs], axis=2),
        jnp.stack([theirs, mine], axis=2),
    ).reshape(tok_rows, 3 * D)
    queries = full[:, :D].reshape(tok_rows, H, DH)
    key_feats = full[:, D : 2 * D].reshape(tok_rows, H, DH)
    values = full[:, 2 * D :].reshape(tok_rows, H, DH)
    local = jnp.einsum(
        "thd,the->hde", key_feats, values, preferred_element_type=jnp.float32
    ).astype(jnp.bfloat16)
    gathered = lax.all_gather(local[None], ("y", "x"), axis=0, tiled=True)
    my_index = lax.axis_index(("y", "x"))
    earlier = (jnp.arange(gathered.shape[0]) < my_index).astype(jnp.bfloat16)
    before = jnp.einsum("c,chde->hde", earlier, gathered, preferred_element_type=jnp.float32)
    memory = prefix_state[0] + before
    attended = span_attention(queries, key_feats, values, memory, head_gain)
    return attended[None]


def solution(mesh):
    n_dp, n_seq = mesh.devices.shape
    n_x = int(round(n_seq ** 0.5))
    split = Mesh(mesh.devices.reshape(n_dp // 2, 2, n_seq // n_x, n_x), ("z", "c", "y", "x"))
    rows = ("z", "c")
    cols = ("y", "x")
    placed = (P(rows, cols, None), P(), P(None, ("z", "c", "y", "x")), P(), P(rows, None, None, None))
    return jax.shard_map(
        body, mesh=split, in_specs=placed, out_specs=P(rows, cols, None), check_vma=False
    )
```

```python
import jax
import jax.numpy as jnp
from jax import lax
from jax.sharding import Mesh, PartitionSpec as P

D = 2048
H = 16
DH = 128
BLOCK = 512


epsilon = 1e-05


def feature_map(inputs):
    return jnp.where(inputs > 0, inputs + 1.0, jnp.exp(jnp.minimum(inputs, 0.0)))


def span_attention(queries, key_feats, values, memory, head_gain):
    num_blocks = queries.shape[0] // BLOCK
    causal = jnp.arange(BLOCK)[:, None] >= jnp.arange(BLOCK)[None, :]
    gains = head_gain.astype(jnp.float32).reshape(H, DH)

    def advance(running, blocks):
        query_blk, key_blk, value_blk = blocks
        carried = jnp.einsum(
            "bhd,hde->bhe",
            query_blk,
            running.astype(jnp.bfloat16),
            preferred_element_type=jnp.float32,
        )
        scores = jnp.einsum("bhd,chd->hbc", query_blk, key_blk, preferred_element_type=jnp.float32)
        scores = jnp.where(causal[None], scores, 0.0).astype(jnp.bfloat16)
        within = jnp.einsum("hbc,che->bhe", scores, value_blk, preferred_element_type=jnp.float32)
        numerator = carried + within
        scale = lax.rsqrt(jnp.mean(numerator * numerator, axis=-1, keepdims=True) + epsilon)
        running = running + jnp.einsum(
            "bhd,bhe->hde", key_blk, value_blk, preferred_element_type=jnp.float32
        )
        return (running, (numerator * scale * gains).astype(jnp.bfloat16))

    def shaped(inputs):
        return inputs.reshape(num_blocks, BLOCK, H, DH)

    final_memory, outputs = lax.scan(
        advance, memory, (shaped(queries), shaped(key_feats), shaped(values))
    )
    return outputs.reshape(num_blocks * BLOCK, H * DH)


def body(tokens, input_gain, qkv_weight, head_gain, prefix_state):
    inputs = tokens[0].astype(jnp.float32)
    normed = inputs * lax.rsqrt(jnp.mean(inputs * inputs, axis=-1, keepdims=True) + epsilon)
    normed = (normed * input_gain.astype(jnp.float32)).astype(jnp.bfloat16)
    tok_rows = normed.shape[0]
    weight = lax.all_gather(qkv_weight, ("dp", "y", "x"), axis=1, tiled=True)
    kv = jnp.dot(normed, weight[:, D:], preferred_element_type=jnp.float32)
    key_feats = feature_map(kv[:, :D]).astype(jnp.bfloat16).reshape(tok_rows, H, DH)
    values = kv[:, D:].astype(jnp.bfloat16).reshape(tok_rows, H, DH)
    local = jnp.einsum(
        "thd,the->hde", key_feats, values, preferred_element_type=jnp.float32
    ).astype(jnp.bfloat16)
    row = lax.all_gather(local, "x", axis=0).astype(jnp.float32)
    x_here = lax.axis_index("x")
    y_here = lax.axis_index("y")
    row_before = jnp.sum(jnp.where((jnp.arange(row.shape[0]) < x_here)[:, None, None, None], row, 0.0), axis=0)
    row_total = jnp.sum(row, axis=0)
    totals = lax.all_gather(row_total, "y", axis=0)
    rows_before = jnp.sum(jnp.where((jnp.arange(totals.shape[0]) < y_here)[:, None, None, None], totals, 0.0), axis=0)
    memory = prefix_state[0] + (rows_before + row_before)
    q = jnp.dot(normed, weight[:, :D], preferred_element_type=jnp.float32)
    queries = feature_map(q).astype(jnp.bfloat16).reshape(tok_rows, H, DH)
    attended = span_attention(queries, key_feats, values, memory, head_gain)
    return attended[None]


def solution(mesh):
    n_dp, n_seq = mesh.devices.shape
    n_x = int(round(n_seq ** 0.5))
    split = Mesh(mesh.devices.reshape(n_dp, n_seq // n_x, n_x), ("dp", "y", "x"))
    cols = ("y", "x")
    placed = (P("dp", cols, None), P(), P(None, ("dp", "y", "x")), P(), P("dp", None, None, None))
    return jax.shard_map(
        body, mesh=split, in_specs=placed, out_specs=P("dp", cols, None), check_vma=False
    )
```

```python
import jax
import jax.numpy as jnp
from jax import lax
from jax.sharding import Mesh, PartitionSpec as P

D = 2048
H = 16
DH = 128
BLOCK = 512


epsilon = 1e-05


def feature_map(inputs):
    return jnp.where(inputs > 0, inputs + 1.0, jnp.exp(jnp.minimum(inputs, 0.0)))


def span_attention(queries, key_feats, values, memory, head_gain):
    num_blocks = queries.shape[0] // BLOCK
    causal = jnp.arange(BLOCK)[:, None] >= jnp.arange(BLOCK)[None, :]
    gains = head_gain.astype(jnp.float32).reshape(H, DH)

    def advance(running, blocks):
        query_blk, key_blk, value_blk = blocks
        carried = jnp.einsum(
            "bhd,hde->bhe",
            query_blk,
            running.astype(jnp.bfloat16),
            preferred_element_type=jnp.float32,
        )
        scores = jnp.einsum("bhd,chd->hbc", query_blk, key_blk, preferred_element_type=jnp.float32)
        scores = jnp.where(causal[None], scores, 0.0).astype(jnp.bfloat16)
        within = jnp.einsum("hbc,che->bhe", scores, value_blk, preferred_element_type=jnp.float32)
        numerator = carried + within
        scale = lax.rsqrt(jnp.mean(numerator * numerator, axis=-1, keepdims=True) + epsilon)
        running = running + jnp.einsum(
            "bhd,bhe->hde", key_blk, value_blk, preferred_element_type=jnp.float32
        )
        return (running, (numerator * scale * gains).astype(jnp.bfloat16))

    def shaped(inputs):
        return inputs.reshape(num_blocks, BLOCK, H, DH)

    final_memory, outputs = lax.scan(
        advance, memory, (shaped(queries), shaped(key_feats), shaped(values))
    )
    return outputs.reshape(num_blocks * BLOCK, H * DH)


def body(tokens, input_gain, qkv_weight, head_gain, prefix_state):
    inputs = tokens[0].astype(jnp.float32)
    normed = inputs * lax.rsqrt(jnp.mean(inputs * inputs, axis=-1, keepdims=True) + epsilon)
    normed = (normed * input_gain.astype(jnp.float32)).astype(jnp.bfloat16)
    tok_rows = normed.shape[0]
    weight = lax.all_gather(qkv_weight, ("dp", "y", "x"), axis=1, tiled=True)
    n_half = 2
    per = D // n_half
    seq_here = lax.axis_index(("y", "x"))
    keys, vals, mems = [], [], []
    for g in range(n_half):
        lo = g * per
        k_g = jnp.dot(normed, weight[:, D + lo : D + lo + per], preferred_element_type=jnp.float32)
        v_g = jnp.dot(normed, weight[:, 2 * D + lo : 2 * D + lo + per], preferred_element_type=jnp.float32)
        k_g = feature_map(k_g).astype(jnp.bfloat16).reshape(tok_rows, per // DH, DH)
        v_g = v_g.astype(jnp.bfloat16).reshape(tok_rows, per // DH, DH)
        local = jnp.einsum(
            "thd,the->hde", k_g, v_g, preferred_element_type=jnp.float32
        ).astype(jnp.bfloat16)
        gathered = lax.all_gather(local[None], ("y", "x"), axis=0, tiled=True)
        earlier = (jnp.arange(gathered.shape[0]) < seq_here).astype(jnp.bfloat16)
        mems.append(jnp.einsum("c,chde->hde", earlier, gathered, preferred_element_type=jnp.float32))
        keys.append(k_g)
        vals.append(v_g)
    key_feats = jnp.concatenate(keys, axis=1)
    values = jnp.concatenate(vals, axis=1)
    memory = prefix_state[0] + jnp.concatenate(mems, axis=0)
    q = jnp.dot(normed, weight[:, :D], preferred_element_type=jnp.float32)
    queries = feature_map(q).astype(jnp.bfloat16).reshape(tok_rows, H, DH)
    attended = span_attention(queries, key_feats, values, memory, head_gain)
    return attended[None]


def solution(mesh):
    n_dp, n_seq = mesh.devices.shape
    n_x = int(round(n_seq ** 0.5))
    split = Mesh(mesh.devices.reshape(n_dp, n_seq // n_x, n_x), ("dp", "y", "x"))
    cols = ("y", "x")
    placed = (P("dp", cols, None), P(), P(None, ("dp", "y", "x")), P(), P("dp", None, None, None))
    return jax.shard_map(
        body, mesh=split, in_specs=placed, out_specs=P("dp", cols, None), check_vma=False
    )
```

```python
import jax
import jax.numpy as jnp
from jax import lax
from jax.sharding import Mesh, PartitionSpec as P

D = 2048
H = 16
DH = 128
BLOCK = 512


epsilon = 1e-05


def feature_map(inputs):
    return jnp.where(inputs > 0, inputs + 1.0, jnp.exp(jnp.minimum(inputs, 0.0)))


def body(tokens, input_gain, qkv_weight, head_gain, prefix_state):
    inputs = tokens[0].astype(jnp.float32)
    normed = inputs * lax.rsqrt(jnp.mean(inputs * inputs, axis=-1, keepdims=True) + epsilon)
    normed = (normed * input_gain.astype(jnp.float32)).astype(jnp.bfloat16)
    tok_rows = normed.shape[0]
    weight = lax.all_gather(qkv_weight, ("dp", "y", "x"), axis=1, tiled=True)
    keys_t = lax.dot_general(
        weight[:, D : 2 * D], normed, (((0,), (1,)), ((), ())), preferred_element_type=jnp.float32
    )
    keys_t = feature_map(keys_t).astype(jnp.bfloat16).reshape(H, DH, tok_rows)
    values = jnp.dot(normed, weight[:, 2 * D :], preferred_element_type=jnp.float32)
    values = values.astype(jnp.bfloat16).reshape(tok_rows, H, DH)
    local = jnp.einsum(
        "hdt,the->hde", keys_t, values, preferred_element_type=jnp.float32
    ).astype(jnp.bfloat16)
    gathered = lax.all_gather(local[None], ("y", "x"), axis=0, tiled=True)
    seq_here = lax.axis_index(("y", "x"))
    earlier = (jnp.arange(gathered.shape[0]) < seq_here).astype(jnp.bfloat16)
    before = jnp.einsum("c,chde->hde", earlier, gathered, preferred_element_type=jnp.float32)
    memory = prefix_state[0] + before
    queries = jnp.dot(normed, weight[:, :D], preferred_element_type=jnp.float32)
    queries = feature_map(queries).astype(jnp.bfloat16).reshape(tok_rows, H, DH)

    causal = jnp.arange(tok_rows)[:, None] >= jnp.arange(tok_rows)[None, :]
    gains = head_gain.astype(jnp.float32).reshape(H, DH)
    scores = jnp.einsum("bhd,hdc->hbc", queries, keys_t, preferred_element_type=jnp.float32)
    scores = jnp.where(causal[None], scores, 0.0).astype(jnp.bfloat16)
    within = jnp.einsum("hbc,che->bhe", scores, values, preferred_element_type=jnp.float32)
    carried = jnp.einsum(
        "bhd,hde->bhe", queries, memory.astype(jnp.bfloat16), preferred_element_type=jnp.float32
    )
    numerator = carried + within
    scale = lax.rsqrt(jnp.mean(numerator * numerator, axis=-1, keepdims=True) + epsilon)
    attended = (numerator * scale * gains).astype(jnp.bfloat16)
    return attended.reshape(1, tok_rows, H * DH)


def solution(mesh):
    n_dp, n_seq = mesh.devices.shape
    n_x = int(round(n_seq ** 0.5))
    split = Mesh(mesh.devices.reshape(n_dp, n_seq // n_x, n_x), ("dp", "y", "x"))
    cols = ("y", "x")
    placed = (P("dp", cols, None), P(), P(None, ("dp", "y", "x")), P(), P("dp", None, None, None))
    return jax.shard_map(
        body, mesh=split, in_specs=placed, out_specs=P("dp", cols, None), check_vma=False
    )
```

```python
import jax
import jax.numpy as jnp
from jax import lax
from jax.experimental import pallas as pl
from jax.sharding import Mesh, PartitionSpec as P

D = 2048
H = 16
DH = 128
BLOCK = 512


epsilon = 1e-05


def feature_map(inputs):
    return jnp.where(inputs > 0, inputs + 1.0, jnp.exp(jnp.minimum(inputs, 0.0)))


def kv_memory_kernel(x_ref, wk_ref, wv_ref, k_ref, v_ref, m_ref):
    x = x_ref[...]
    dims = (((1,), (1,)), ((), ()))
    k = lax.dot_general(x, wk_ref[...], dims, preferred_element_type=jnp.float32)
    k = feature_map(k).astype(jnp.bfloat16)
    v = lax.dot_general(x, wv_ref[...], dims, preferred_element_type=jnp.float32).astype(jnp.bfloat16)
    k_ref[...] = k
    v_ref[...] = v
    for j in range(m_ref.shape[0]):
        part = slice(j * DH, (j + 1) * DH)
        m = lax.dot_general(k[:, part], v[:, part], (((0,), (0,)), ((), ())), preferred_element_type=jnp.float32)
        m_ref[j] = m.astype(jnp.bfloat16)


def kv_memory(normed, weight_t, heads_per_step=2):
    rows = normed.shape[0]
    width = heads_per_step * DH
    k_off = D // width
    v_off = 2 * D // width
    return pl.pallas_call(
        kv_memory_kernel,
        grid=(H // heads_per_step,),
        in_specs=[
            pl.BlockSpec((rows, D), lambda i: (0, 0)),
            pl.BlockSpec((width, D), lambda i: (k_off + i, 0)),
            pl.BlockSpec((width, D), lambda i: (v_off + i, 0)),
        ],
        out_specs=[
            pl.BlockSpec((rows, width), lambda i: (0, i)),
            pl.BlockSpec((rows, width), lambda i: (0, i)),
            pl.BlockSpec((heads_per_step, DH, DH), lambda i: (i, 0, 0)),
        ],
        out_shape=[
            jax.ShapeDtypeStruct((rows, D), jnp.bfloat16),
            jax.ShapeDtypeStruct((rows, D), jnp.bfloat16),
            jax.ShapeDtypeStruct((H, DH, DH), jnp.bfloat16),
        ],
    )(normed, weight_t, weight_t)


def body(tokens, input_gain, qkv_weight, head_gain, prefix_state):
    inputs = tokens[0].astype(jnp.float32)
    normed = inputs * lax.rsqrt(jnp.mean(inputs * inputs, axis=-1, keepdims=True) + epsilon)
    normed = (normed * input_gain.astype(jnp.float32)).astype(jnp.bfloat16)
    tok_rows = normed.shape[0]
    weight = lax.all_gather(qkv_weight, ("dp", "y", "x"), axis=1, tiled=True)
    key_feats, values, local = kv_memory(normed, weight.T)
    key_feats = key_feats.reshape(tok_rows, H, DH)
    values = values.reshape(tok_rows, H, DH)
    gathered = lax.all_gather(local[None], ("y", "x"), axis=0, tiled=True)
    seq_here = lax.axis_index(("y", "x"))
    earlier = (jnp.arange(gathered.shape[0]) < seq_here).astype(jnp.bfloat16)
    before = jnp.einsum("c,chde->hde", earlier, gathered, preferred_element_type=jnp.float32)
    memory = prefix_state[0] + before
    queries = jnp.dot(normed, weight[:, :D], preferred_element_type=jnp.float32)
    queries = feature_map(queries).astype(jnp.bfloat16).reshape(tok_rows, H, DH)

    causal = jnp.arange(tok_rows)[:, None] >= jnp.arange(tok_rows)[None, :]
    gains = head_gain.astype(jnp.float32).reshape(H, DH)
    scores = jnp.einsum("bhd,chd->hbc", queries, key_feats, preferred_element_type=jnp.float32)
    scores = jnp.where(causal[None], scores, 0.0).astype(jnp.bfloat16)
    within = jnp.einsum("hbc,che->bhe", scores, values, preferred_element_type=jnp.float32)
    carried = jnp.einsum(
        "bhd,hde->bhe", queries, memory.astype(jnp.bfloat16), preferred_element_type=jnp.float32
    )
    numerator = carried + within
    scale = lax.rsqrt(jnp.mean(numerator * numerator, axis=-1, keepdims=True) + epsilon)
    attended = (numerator * scale * gains).astype(jnp.bfloat16)
    return attended.reshape(1, tok_rows, H * DH)


def solution(mesh):
    n_dp, n_seq = mesh.devices.shape
    n_x = int(round(n_seq ** 0.5))
    split = Mesh(mesh.devices.reshape(n_dp, n_seq // n_x, n_x), ("dp", "y", "x"))
    cols = ("y", "x")
    placed = (P("dp", cols, None), P(), P(None, ("dp", "y", "x")), P(), P("dp", None, None, None))
    return jax.shard_map(
        body, mesh=split, in_specs=placed, out_specs=P("dp", cols, None), check_vma=False
    )
```

```python
import jax
import jax.numpy as jnp
from jax import lax
from jax.experimental import pallas as pl
from jax.experimental.pallas import tpu as pltpu
from jax.sharding import Mesh, PartitionSpec as P

D = 2048
H = 16
DH = 128
BLOCK = 512


epsilon = 1e-05


def feature_map(inputs):
    return jnp.where(inputs > 0, inputs + 1.0, jnp.exp(jnp.minimum(inputs, 0.0)))


def kv_memory_kernel(x_ref, wk_ref, wv_ref, k_ref, v_ref, m_ref):
    x = x_ref[...]
    dims = (((1,), (1,)), ((), ()))
    k = lax.dot_general(x, wk_ref[...], dims, preferred_element_type=jnp.float32)
    k = feature_map(k).astype(jnp.bfloat16)
    v = lax.dot_general(x, wv_ref[...], dims, preferred_element_type=jnp.float32).astype(jnp.bfloat16)
    k_ref[...] = k
    v_ref[...] = v
    for j in range(m_ref.shape[0]):
        part = slice(j * DH, (j + 1) * DH)
        m = lax.dot_general(k[:, part], v[:, part], (((0,), (0,)), ((), ())), preferred_element_type=jnp.float32)
        m_ref[j] = m.astype(jnp.bfloat16)


def kv_memory(normed, weight_t, heads_per_step=2):
    rows = normed.shape[0]
    width = heads_per_step * DH
    k_off = D // width
    v_off = 2 * D // width
    return pl.pallas_call(
        kv_memory_kernel,
        grid=(H // heads_per_step,),
        in_specs=[
            pl.BlockSpec((rows, D), lambda i: (0, 0)),
            pl.BlockSpec((width, D), lambda i: (k_off + i, 0)),
            pl.BlockSpec((width, D), lambda i: (v_off + i, 0)),
        ],
        out_specs=[
            pl.BlockSpec((rows, width), lambda i: (0, i)),
            pl.BlockSpec((rows, width), lambda i: (0, i)),
            pl.BlockSpec((heads_per_step, DH, DH), lambda i: (i, 0, 0)),
        ],
        out_shape=[
            jax.ShapeDtypeStruct((rows, D), jnp.bfloat16),
            jax.ShapeDtypeStruct((rows, D), jnp.bfloat16),
            jax.ShapeDtypeStruct((H, DH, DH), jnp.bfloat16),
        ],
    )(normed, weight_t, weight_t)


def tail_kernel(here_ref, g_ref, p_ref, q_ref, w_ref, gain_ref, o_ref):
    here = here_ref[0]
    for j in range(p_ref.shape[0]):
        state = p_ref[j]
        for c in range(g_ref.shape[0]):
            state = state + jnp.where(c < here, g_ref[c, j].astype(jnp.float32), 0.0)
        part = slice(j * DH, (j + 1) * DH)
        carried = jnp.dot(q_ref[:, part], state.astype(jnp.bfloat16), preferred_element_type=jnp.float32)
        numerator = carried + w_ref[:, part]
        scale = lax.rsqrt(jnp.mean(numerator * numerator, axis=-1, keepdims=True) + epsilon)
        o_ref[:, part] = (numerator * scale * gain_ref[:, part]).astype(o_ref.dtype)


def attend_tail(here, gathered, prefix, queries, within, gains, heads_per_step=2):
    rows = queries.shape[0]
    n_piece = gathered.shape[0]
    width = heads_per_step * DH
    grid_spec = pltpu.PrefetchScalarGridSpec(
        num_scalar_prefetch=1,
        grid=(H // heads_per_step,),
        in_specs=[
            pl.BlockSpec((n_piece, heads_per_step, DH, DH), lambda i, s: (0, i, 0, 0)),
            pl.BlockSpec((heads_per_step, DH, DH), lambda i, s: (i, 0, 0)),
            pl.BlockSpec((rows, width), lambda i, s: (0, i)),
            pl.BlockSpec((rows, width), lambda i, s: (0, i)),
            pl.BlockSpec((1, width), lambda i, s: (0, i)),
        ],
        out_specs=pl.BlockSpec((rows, width), lambda i, s: (0, i)),
    )
    return pl.pallas_call(
        tail_kernel,
        grid_spec=grid_spec,
        out_shape=jax.ShapeDtypeStruct((rows, H * DH), jnp.bfloat16),
    )(here, gathered, prefix, queries, within, gains)


def body(tokens, input_gain, qkv_weight, head_gain, prefix_state):
    inputs = tokens[0].astype(jnp.float32)
    normed = inputs * lax.rsqrt(jnp.mean(inputs * inputs, axis=-1, keepdims=True) + epsilon)
    normed = (normed * input_gain.astype(jnp.float32)).astype(jnp.bfloat16)
    tok_rows = normed.shape[0]
    weight = lax.all_gather(qkv_weight, ("dp", "y", "x"), axis=1, tiled=True)
    key_feats, values, local = kv_memory(normed, weight.T)
    key_feats = key_feats.reshape(tok_rows, H, DH)
    values = values.reshape(tok_rows, H, DH)
    gathered = lax.all_gather(local[None], ("y", "x"), axis=0, tiled=True)
    seq_here = lax.axis_index(("y", "x")).astype(jnp.int32).reshape(1)
    queries = jnp.dot(normed, weight[:, :D], preferred_element_type=jnp.float32)
    queries = feature_map(queries).astype(jnp.bfloat16)

    causal = jnp.arange(tok_rows)[:, None] >= jnp.arange(tok_rows)[None, :]
    scores = jnp.einsum(
        "bhd,chd->hbc", queries.reshape(tok_rows, H, DH), key_feats, preferred_element_type=jnp.float32
    )
    scores = jnp.where(causal[None], scores, 0.0).astype(jnp.bfloat16)
    within = jnp.einsum("hbc,che->bhe", scores, values, preferred_element_type=jnp.float32)
    gains = head_gain.astype(jnp.float32).reshape(1, H * DH)
    attended = attend_tail(
        seq_here, gathered, prefix_state[0], queries, within.reshape(tok_rows, H * DH), gains
    )
    return attended.reshape(1, tok_rows, H * DH)


def solution(mesh):
    n_dp, n_seq = mesh.devices.shape
    n_x = int(round(n_seq ** 0.5))
    split = Mesh(mesh.devices.reshape(n_dp, n_seq // n_x, n_x), ("dp", "y", "x"))
    cols = ("y", "x")
    placed = (P("dp", cols, None), P(), P(None, ("dp", "y", "x")), P(), P("dp", None, None, None))
    return jax.shard_map(
        body, mesh=split, in_specs=placed, out_specs=P("dp", cols, None), check_vma=False
    )
```

```python
import jax
import jax.numpy as jnp
from jax import lax
from jax.experimental import pallas as pl
from jax.experimental.pallas import tpu as pltpu
from jax.sharding import Mesh, PartitionSpec as P

D = 2048
H = 16
DH = 128
BLOCK = 512


epsilon = 1e-05


def feature_map(inputs):
    return jnp.where(inputs > 0, inputs + 1.0, jnp.exp(jnp.minimum(inputs, 0.0)))


def kv_memory_kernel(x_ref, wk_ref, wv_ref, k_ref, v_ref, m_ref):
    x = x_ref[...]
    dims = (((1,), (1,)), ((), ()))
    k = lax.dot_general(x, wk_ref[...], dims, preferred_element_type=jnp.float32)
    k = feature_map(k).astype(jnp.bfloat16)
    v = lax.dot_general(x, wv_ref[...], dims, preferred_element_type=jnp.float32).astype(jnp.bfloat16)
    k_ref[...] = k
    v_ref[...] = v
    for j in range(m_ref.shape[0]):
        part = slice(j * DH, (j + 1) * DH)
        m = lax.dot_general(k[:, part], v[:, part], (((0,), (0,)), ((), ())), preferred_element_type=jnp.float32)
        m_ref[j] = m.astype(jnp.bfloat16)


def kv_memory(normed, weight_t, heads_per_step=2):
    rows = normed.shape[0]
    width = heads_per_step * DH
    k_off = D // width
    v_off = 2 * D // width
    return pl.pallas_call(
        kv_memory_kernel,
        grid=(H // heads_per_step,),
        in_specs=[
            pl.BlockSpec((rows, D), lambda i: (0, 0)),
            pl.BlockSpec((width, D), lambda i: (k_off + i, 0)),
            pl.BlockSpec((width, D), lambda i: (v_off + i, 0)),
        ],
        out_specs=[
            pl.BlockSpec((rows, width), lambda i: (0, i)),
            pl.BlockSpec((rows, width), lambda i: (0, i)),
            pl.BlockSpec((heads_per_step, DH, DH), lambda i: (i, 0, 0)),
        ],
        out_shape=[
            jax.ShapeDtypeStruct((rows, D), jnp.bfloat16),
            jax.ShapeDtypeStruct((rows, D), jnp.bfloat16),
            jax.ShapeDtypeStruct((H, DH, DH), jnp.bfloat16),
        ],
    )(normed, weight_t, weight_t)


def tail_kernel(sel_ref, g_ref, p_ref, q_ref, w_ref, gain_ref, o_ref):
    sel = sel_ref[...]
    for j in range(p_ref.shape[0]):
        state = p_ref[j] + jnp.dot(sel, g_ref[j], preferred_element_type=jnp.float32)
        part = slice(j * DH, (j + 1) * DH)
        carried = jnp.dot(q_ref[:, part], state.astype(jnp.bfloat16), preferred_element_type=jnp.float32)
        numerator = carried + w_ref[:, part]
        scale = lax.rsqrt(jnp.mean(numerator * numerator, axis=-1, keepdims=True) + epsilon)
        o_ref[:, part] = (numerator * scale * gain_ref[:, part]).astype(o_ref.dtype)


def attend_tail(select, gathered, prefix, queries, within, gains, heads_per_step=2):
    rows = queries.shape[0]
    stack = gathered.shape[1]
    width = heads_per_step * DH
    return pl.pallas_call(
        tail_kernel,
        grid=(H // heads_per_step,),
        in_specs=[
            pl.BlockSpec((DH, stack), lambda i: (0, 0)),
            pl.BlockSpec((heads_per_step, stack, DH), lambda i: (i, 0, 0)),
            pl.BlockSpec((heads_per_step, DH, DH), lambda i: (i, 0, 0)),
            pl.BlockSpec((rows, width), lambda i: (0, i)),
            pl.BlockSpec((rows, width), lambda i: (0, i)),
            pl.BlockSpec((1, width), lambda i: (0, i)),
        ],
        out_specs=pl.BlockSpec((rows, width), lambda i: (0, i)),
        out_shape=jax.ShapeDtypeStruct((rows, H * DH), jnp.bfloat16),
    )(select, gathered, prefix, queries, within, gains)


def body(tokens, input_gain, qkv_weight, head_gain, prefix_state):
    inputs = tokens[0].astype(jnp.float32)
    normed = inputs * lax.rsqrt(jnp.mean(inputs * inputs, axis=-1, keepdims=True) + epsilon)
    normed = (normed * input_gain.astype(jnp.float32)).astype(jnp.bfloat16)
    tok_rows = normed.shape[0]
    weight = lax.all_gather(qkv_weight, ("dp", "y", "x"), axis=1, tiled=True)
    key_feats, values, local = kv_memory(normed, weight.T)
    key_feats = key_feats.reshape(tok_rows, H, DH)
    values = values.reshape(tok_rows, H, DH)
    gathered = lax.all_gather(local, ("y", "x"), axis=1, tiled=True)
    seq_here = lax.axis_index(("y", "x"))
    sel_row = jnp.arange(DH)[:, None]
    sel_col = jnp.arange(gathered.shape[1])[None, :]
    select = ((sel_col % DH == sel_row) & (sel_col // DH < seq_here)).astype(jnp.bfloat16)
    queries = jnp.dot(normed, weight[:, :D], preferred_element_type=jnp.float32)
    queries = feature_map(queries).astype(jnp.bfloat16)

    causal = jnp.arange(tok_rows)[:, None] >= jnp.arange(tok_rows)[None, :]
    scores = jnp.einsum(
        "bhd,chd->hbc", queries.reshape(tok_rows, H, DH), key_feats, preferred_element_type=jnp.float32
    )
    scores = jnp.where(causal[None], scores, 0.0).astype(jnp.bfloat16)
    within = jnp.einsum("hbc,che->bhe", scores, values, preferred_element_type=jnp.float32)
    gains = head_gain.astype(jnp.float32).reshape(1, H * DH)
    attended = attend_tail(
        select, gathered, prefix_state[0], queries, within.reshape(tok_rows, H * DH), gains
    )
    return attended.reshape(1, tok_rows, H * DH)


def solution(mesh):
    n_dp, n_seq = mesh.devices.shape
    n_x = int(round(n_seq ** 0.5))
    split = Mesh(mesh.devices.reshape(n_dp, n_seq // n_x, n_x), ("dp", "y", "x"))
    cols = ("y", "x")
    placed = (P("dp", cols, None), P(), P(None, ("dp", "y", "x")), P(), P("dp", None, None, None))
    return jax.shard_map(
        body, mesh=split, in_specs=placed, out_specs=P("dp", cols, None), check_vma=False
    )
```

```python
import jax
import jax.numpy as jnp
from jax import lax
from jax.experimental import pallas as pl
from jax.sharding import Mesh, PartitionSpec as P

D = 2048
H = 16
DH = 128
BLOCK = 512


epsilon = 1e-05


def feature_map(inputs):
    return jnp.where(inputs > 0, inputs + 1.0, jnp.exp(jnp.minimum(inputs, 0.0)))


def kv_memory_kernel(x_ref, wk_ref, wv_ref, k_ref, v_ref, m_ref):
    x = x_ref[...]
    dims = (((1,), (1,)), ((), ()))
    k = lax.dot_general(x, wk_ref[...], dims, preferred_element_type=jnp.float32)
    k = feature_map(k).astype(jnp.bfloat16)
    v = lax.dot_general(x, wv_ref[...], dims, preferred_element_type=jnp.float32).astype(jnp.bfloat16)
    k_ref[...] = k
    v_ref[...] = v
    for j in range(m_ref.shape[0]):
        part = slice(j * DH, (j + 1) * DH)
        m = lax.dot_general(k[:, part], v[:, part], (((0,), (0,)), ((), ())), preferred_element_type=jnp.float32)
        m_ref[j] = m.astype(jnp.bfloat16)


def kv_memory(normed, weight_t, heads_per_step=2):
    rows = normed.shape[0]
    width = heads_per_step * DH
    k_off = D // width
    v_off = 2 * D // width
    return pl.pallas_call(
        kv_memory_kernel,
        grid=(H // heads_per_step,),
        in_specs=[
            pl.BlockSpec((rows, D), lambda i: (0, 0)),
            pl.BlockSpec((width, D), lambda i: (k_off + i, 0)),
            pl.BlockSpec((width, D), lambda i: (v_off + i, 0)),
        ],
        out_specs=[
            pl.BlockSpec((rows, width), lambda i: (0, i)),
            pl.BlockSpec((rows, width), lambda i: (0, i)),
            pl.BlockSpec((heads_per_step, DH, DH), lambda i: (i, 0, 0)),
        ],
        out_shape=[
            jax.ShapeDtypeStruct((rows, D), jnp.bfloat16),
            jax.ShapeDtypeStruct((rows, D), jnp.bfloat16),
            jax.ShapeDtypeStruct((H, DH, DH), jnp.bfloat16),
        ],
    )(normed, weight_t, weight_t)


def body(tokens, input_gain, qkv_weight, head_gain, prefix_state):
    inputs = tokens[0].astype(jnp.float32)
    normed = inputs * lax.rsqrt(jnp.mean(inputs * inputs, axis=-1, keepdims=True) + epsilon)
    normed = (normed * input_gain.astype(jnp.float32)).astype(jnp.bfloat16)
    tok_rows = normed.shape[0]
    weight = lax.all_gather(qkv_weight, ("dp", "y", "x"), axis=1, tiled=True)
    key_feats, values, local = kv_memory(normed, weight.T)
    key_feats = key_feats.reshape(tok_rows, H, DH)
    values = values.reshape(tok_rows, H, DH)
    gathered = lax.all_gather(local, ("y", "x"), axis=1, tiled=True)
    seq_here = lax.axis_index(("y", "x"))
    sel_row = jnp.arange(DH)[:, None]
    sel_col = jnp.arange(gathered.shape[1])[None, :]
    select = ((sel_col % DH == sel_row) & (sel_col // DH < seq_here)).astype(jnp.bfloat16)
    before = jnp.einsum("rc,hce->hre", select, gathered, preferred_element_type=jnp.float32)
    memory = prefix_state[0] + before
    queries = jnp.dot(normed, weight[:, :D], preferred_element_type=jnp.float32)
    queries = feature_map(queries).astype(jnp.bfloat16).reshape(tok_rows, H, DH)

    causal = jnp.arange(tok_rows)[:, None] >= jnp.arange(tok_rows)[None, :]
    gains = head_gain.astype(jnp.float32).reshape(H, DH)
    scores = jnp.einsum("bhd,chd->hbc", queries, key_feats, preferred_element_type=jnp.float32)
    scores = jnp.where(causal[None], scores, 0.0).astype(jnp.bfloat16)
    within = jnp.einsum("hbc,che->bhe", scores, values, preferred_element_type=jnp.float32)
    carried = jnp.einsum(
        "bhd,hde->bhe", queries, memory.astype(jnp.bfloat16), preferred_element_type=jnp.float32
    )
    numerator = carried + within
    scale = lax.rsqrt(jnp.mean(numerator * numerator, axis=-1, keepdims=True) + epsilon)
    attended = (numerator * scale * gains).astype(jnp.bfloat16)
    return attended.reshape(1, tok_rows, H * DH)


def solution(mesh):
    n_dp, n_seq = mesh.devices.shape
    n_x = int(round(n_seq ** 0.5))
    split = Mesh(mesh.devices.reshape(n_dp, n_seq // n_x, n_x), ("dp", "y", "x"))
    cols = ("y", "x")
    placed = (P("dp", cols, None), P(), P(None, ("dp", "y", "x")), P(), P("dp", None, None, None))
    return jax.shard_map(
        body, mesh=split, in_specs=placed, out_specs=P("dp", cols, None), check_vma=False
    )
```

```python
import jax
import jax.numpy as jnp
from jax import lax
from jax.experimental import pallas as pl
from jax.experimental.pallas import tpu as pltpu
from jax.sharding import Mesh, PartitionSpec as P

D = 2048
H = 16
DH = 128
BLOCK = 512


epsilon = 1e-05


def feature_map(inputs):
    return jnp.where(inputs > 0, inputs + 1.0, jnp.exp(jnp.minimum(inputs, 0.0)))


def kv_memory_kernel(x_ref, wk_ref, wv_ref, k_ref, v_ref, m_ref):
    x = x_ref[...]
    dims = (((1,), (1,)), ((), ()))
    k = lax.dot_general(x, wk_ref[...], dims, preferred_element_type=jnp.float32)
    k = feature_map(k).astype(jnp.bfloat16)
    v = lax.dot_general(x, wv_ref[...], dims, preferred_element_type=jnp.float32).astype(jnp.bfloat16)
    k_ref[...] = k
    v_ref[...] = v
    for j in range(m_ref.shape[0]):
        part = slice(j * DH, (j + 1) * DH)
        m = lax.dot_general(k[:, part], v[:, part], (((0,), (0,)), ((), ())), preferred_element_type=jnp.float32)
        m_ref[j] = m.astype(jnp.bfloat16)


def kv_memory(normed, weight_t, heads_per_step=2):
    rows = normed.shape[0]
    width = heads_per_step * DH
    k_off = D // width
    v_off = 2 * D // width
    return pl.pallas_call(
        kv_memory_kernel,
        grid=(H // heads_per_step,),
        in_specs=[
            pl.BlockSpec((rows, D), lambda i: (0, 0)),
            pl.BlockSpec((width, D), lambda i: (k_off + i, 0)),
            pl.BlockSpec((width, D), lambda i: (v_off + i, 0)),
        ],
        out_specs=[
            pl.BlockSpec((rows, width), lambda i: (0, i)),
            pl.BlockSpec((rows, width), lambda i: (0, i)),
            pl.BlockSpec((heads_per_step, DH, DH), lambda i: (i, 0, 0)),
        ],
        out_shape=[
            jax.ShapeDtypeStruct((rows, D), jnp.bfloat16),
            jax.ShapeDtypeStruct((rows, D), jnp.bfloat16),
            jax.ShapeDtypeStruct((H, DH, DH), jnp.bfloat16),
        ],
    )(normed, weight_t, weight_t)


def tail_kernel(here_ref, g_ref, p_ref, q_ref, w_ref, gain_ref, o_ref):
    here = here_ref[0]
    for j in range(p_ref.shape[0]):
        state = p_ref[j]
        for c in range(g_ref.shape[0]):
            state = state + jnp.where(c < here, g_ref[c, j].astype(jnp.float32), 0.0)
        carried = jnp.dot(q_ref[j], state.astype(jnp.bfloat16), preferred_element_type=jnp.float32)
        numerator = carried + w_ref[j]
        scale = lax.rsqrt(jnp.mean(numerator * numerator, axis=-1, keepdims=True) + epsilon)
        part = slice(j * DH, (j + 1) * DH)
        o_ref[:, part] = (numerator * scale * gain_ref[:, part]).astype(o_ref.dtype)


def attend_tail(here, gathered, prefix, queries, within, gains, heads_per_step=4):
    rows = queries.shape[1]
    n_piece = gathered.shape[0]
    width = heads_per_step * DH
    grid_spec = pltpu.PrefetchScalarGridSpec(
        num_scalar_prefetch=1,
        grid=(H // heads_per_step,),
        in_specs=[
            pl.BlockSpec((n_piece, heads_per_step, DH, DH), lambda i, s: (0, i, 0, 0)),
            pl.BlockSpec((heads_per_step, DH, DH), lambda i, s: (i, 0, 0)),
            pl.BlockSpec((heads_per_step, rows, DH), lambda i, s: (i, 0, 0)),
            pl.BlockSpec((heads_per_step, rows, DH), lambda i, s: (i, 0, 0)),
            pl.BlockSpec((1, width), lambda i, s: (0, i)),
        ],
        out_specs=pl.BlockSpec((rows, width), lambda i, s: (0, i)),
    )
    return pl.pallas_call(
        tail_kernel,
        grid_spec=grid_spec,
        out_shape=jax.ShapeDtypeStruct((rows, H * DH), jnp.bfloat16),
    )(here, gathered, prefix, queries, within, gains)


def body(tokens, input_gain, qkv_weight, head_gain, prefix_state):
    inputs = tokens[0].astype(jnp.float32)
    normed = inputs * lax.rsqrt(jnp.mean(inputs * inputs, axis=-1, keepdims=True) + epsilon)
    normed = (normed * input_gain.astype(jnp.float32)).astype(jnp.bfloat16)
    tok_rows = normed.shape[0]
    weight = lax.all_gather(qkv_weight, ("dp", "y", "x"), axis=1, tiled=True)
    key_feats, values, local = kv_memory(normed, weight.T)
    key_feats = key_feats.reshape(tok_rows, H, DH)
    values = values.reshape(tok_rows, H, DH)
    gathered = lax.all_gather(local[None], ("y", "x"), axis=0, tiled=True)
    seq_here = lax.axis_index(("y", "x")).astype(jnp.int32).reshape(1)
    queries = jnp.dot(normed, weight[:, :D], preferred_element_type=jnp.float32)
    queries = feature_map(queries).astype(jnp.bfloat16)

    causal = jnp.arange(tok_rows)[:, None] >= jnp.arange(tok_rows)[None, :]
    scores = jnp.einsum(
        "bhd,chd->hbc", queries.reshape(tok_rows, H, DH), key_feats, preferred_element_type=jnp.float32
    )
    scores = jnp.where(causal[None], scores, 0.0).astype(jnp.bfloat16)
    within = jnp.einsum("hbc,che->hbe", scores, values, preferred_element_type=jnp.float32)
    gains = head_gain.astype(jnp.float32).reshape(1, H * DH)
    attended = attend_tail(
        seq_here, gathered, prefix_state[0], jnp.transpose(queries.reshape(tok_rows, H, DH), (1, 0, 2)), within, gains
    )
    return attended.reshape(1, tok_rows, H * DH)


def solution(mesh):
    n_dp, n_seq = mesh.devices.shape
    n_x = int(round(n_seq ** 0.5))
    split = Mesh(mesh.devices.reshape(n_dp, n_seq // n_x, n_x), ("dp", "y", "x"))
    cols = ("y", "x")
    placed = (P("dp", cols, None), P(), P(None, ("dp", "y", "x")), P(), P("dp", None, None, None))
    return jax.shard_map(
        body, mesh=split, in_specs=placed, out_specs=P("dp", cols, None), check_vma=False
    )
```

```python
import jax
import jax.numpy as jnp
from jax import lax
from jax.experimental import pallas as pl
from jax.experimental.pallas import tpu as pltpu
from jax.sharding import Mesh, PartitionSpec as P

D = 2048
H = 16
DH = 128
BLOCK = 512


epsilon = 1e-05


def feature_map(inputs):
    return jnp.where(inputs > 0, inputs + 1.0, jnp.exp(jnp.minimum(inputs, 0.0)))


def kv_memory_kernel(x_ref, wk_ref, wv_ref, k_ref, v_ref, m_ref):
    x = x_ref[...]
    dims = (((1,), (1,)), ((), ()))
    k = lax.dot_general(x, wk_ref[...], dims, preferred_element_type=jnp.float32)
    k = feature_map(k).astype(jnp.bfloat16)
    v = lax.dot_general(x, wv_ref[...], dims, preferred_element_type=jnp.float32).astype(jnp.bfloat16)
    k_ref[...] = k
    v_ref[...] = v
    for j in range(m_ref.shape[0]):
        part = slice(j * DH, (j + 1) * DH)
        m = lax.dot_general(k[:, part], v[:, part], (((0,), (0,)), ((), ())), preferred_element_type=jnp.float32)
        m_ref[j] = m.astype(jnp.bfloat16)


def kv_memory(normed, weight_t, heads_per_step=2):
    rows = normed.shape[0]
    width = heads_per_step * DH
    k_off = D // width
    v_off = 2 * D // width
    return pl.pallas_call(
        kv_memory_kernel,
        grid=(H // heads_per_step,),
        in_specs=[
            pl.BlockSpec((rows, D), lambda i: (0, 0)),
            pl.BlockSpec((width, D), lambda i: (k_off + i, 0)),
            pl.BlockSpec((width, D), lambda i: (v_off + i, 0)),
        ],
        out_specs=[
            pl.BlockSpec((rows, width), lambda i: (0, i)),
            pl.BlockSpec((rows, width), lambda i: (0, i)),
            pl.BlockSpec((heads_per_step, DH, DH), lambda i: (i, 0, 0)),
        ],
        out_shape=[
            jax.ShapeDtypeStruct((rows, D), jnp.bfloat16),
            jax.ShapeDtypeStruct((rows, D), jnp.bfloat16),
            jax.ShapeDtypeStruct((H, DH, DH), jnp.bfloat16),
        ],
    )(normed, weight_t, weight_t)


def tail_kernel(here_ref, g_ref, p_ref, q_ref, w_ref, gain_ref, o_ref):
    here = here_ref[0]
    for j in range(p_ref.shape[0]):
        state = lax.fori_loop(
            0, here, lambda c, acc: acc + g_ref[c, j].astype(jnp.float32), p_ref[j]
        )
        carried = jnp.dot(q_ref[j], state.astype(jnp.bfloat16), preferred_element_type=jnp.float32)
        numerator = carried + w_ref[j]
        scale = lax.rsqrt(jnp.mean(numerator * numerator, axis=-1, keepdims=True) + epsilon)
        part = slice(j * DH, (j + 1) * DH)
        o_ref[:, part] = (numerator * scale * gain_ref[:, part]).astype(o_ref.dtype)


def attend_tail(here, gathered, prefix, queries, within, gains, heads_per_step=4):
    rows = queries.shape[1]
    n_piece = gathered.shape[0]
    width = heads_per_step * DH
    grid_spec = pltpu.PrefetchScalarGridSpec(
        num_scalar_prefetch=1,
        grid=(H // heads_per_step,),
        in_specs=[
            pl.BlockSpec((n_piece, heads_per_step, DH, DH), lambda i, s: (0, i, 0, 0)),
            pl.BlockSpec((heads_per_step, DH, DH), lambda i, s: (i, 0, 0)),
            pl.BlockSpec((heads_per_step, rows, DH), lambda i, s: (i, 0, 0)),
            pl.BlockSpec((heads_per_step, rows, DH), lambda i, s: (i, 0, 0)),
            pl.BlockSpec((1, width), lambda i, s: (0, i)),
        ],
        out_specs=pl.BlockSpec((rows, width), lambda i, s: (0, i)),
    )
    return pl.pallas_call(
        tail_kernel,
        grid_spec=grid_spec,
        out_shape=jax.ShapeDtypeStruct((rows, H * DH), jnp.bfloat16),
    )(here, gathered, prefix, queries, within, gains)


def body(tokens, input_gain, qkv_weight, head_gain, prefix_state):
    inputs = tokens[0].astype(jnp.float32)
    normed = inputs * lax.rsqrt(jnp.mean(inputs * inputs, axis=-1, keepdims=True) + epsilon)
    normed = (normed * input_gain.astype(jnp.float32)).astype(jnp.bfloat16)
    tok_rows = normed.shape[0]
    weight = lax.all_gather(qkv_weight, ("dp", "y", "x"), axis=1, tiled=True)
    key_feats, values, local = kv_memory(normed, weight.T)
    key_feats = key_feats.reshape(tok_rows, H, DH)
    values = values.reshape(tok_rows, H, DH)
    gathered = lax.all_gather(local[None], ("y", "x"), axis=0, tiled=True)
    seq_here = lax.axis_index(("y", "x")).astype(jnp.int32).reshape(1)
    queries = jnp.dot(normed, weight[:, :D], preferred_element_type=jnp.float32)
    queries = feature_map(queries).astype(jnp.bfloat16)

    causal = jnp.arange(tok_rows)[:, None] >= jnp.arange(tok_rows)[None, :]
    scores = jnp.einsum(
        "bhd,chd->hbc", queries.reshape(tok_rows, H, DH), key_feats, preferred_element_type=jnp.float32
    )
    scores = jnp.where(causal[None], scores, 0.0).astype(jnp.bfloat16)
    within = jnp.einsum("hbc,che->hbe", scores, values, preferred_element_type=jnp.float32)
    gains = head_gain.astype(jnp.float32).reshape(1, H * DH)
    attended = attend_tail(
        seq_here, gathered, prefix_state[0], jnp.transpose(queries.reshape(tok_rows, H, DH), (1, 0, 2)), within, gains
    )
    return attended.reshape(1, tok_rows, H * DH)


def solution(mesh):
    n_dp, n_seq = mesh.devices.shape
    n_x = int(round(n_seq ** 0.5))
    split = Mesh(mesh.devices.reshape(n_dp, n_seq // n_x, n_x), ("dp", "y", "x"))
    cols = ("y", "x")
    placed = (P("dp", cols, None), P(), P(None, ("dp", "y", "x")), P(), P("dp", None, None, None))
    return jax.shard_map(
        body, mesh=split, in_specs=placed, out_specs=P("dp", cols, None), check_vma=False
    )
```

```python
import jax
import jax.numpy as jnp
from jax import lax
from jax.experimental import pallas as pl
from jax.sharding import Mesh, PartitionSpec as P

D = 2048
H = 16
DH = 128
BLOCK = 512


epsilon = 1e-05


def feature_map(inputs):
    return jnp.where(inputs > 0, inputs + 1.0, jnp.exp(jnp.minimum(inputs, 0.0)))


def kv_memory_kernel(x_ref, wk_ref, wv_ref, k_ref, v_ref, m_ref):
    x = x_ref[...]
    dims = (((1,), (1,)), ((), ()))
    k = lax.dot_general(x, wk_ref[...], dims, preferred_element_type=jnp.float32)
    k = feature_map(k).astype(jnp.bfloat16)
    v = lax.dot_general(x, wv_ref[...], dims, preferred_element_type=jnp.float32).astype(jnp.bfloat16)
    k_ref[...] = k
    v_ref[...] = v
    for j in range(m_ref.shape[0]):
        part = slice(j * DH, (j + 1) * DH)
        m = lax.dot_general(k[:, part], v[:, part], (((0,), (0,)), ((), ())), preferred_element_type=jnp.float32)
        m_ref[j] = m.astype(jnp.bfloat16)


def kv_memory(normed, weight_t, heads_per_step=2):
    rows = normed.shape[0]
    width = heads_per_step * DH
    k_off = D // width
    v_off = 2 * D // width
    return pl.pallas_call(
        kv_memory_kernel,
        grid=(H // heads_per_step,),
        in_specs=[
            pl.BlockSpec((rows, D), lambda i: (0, 0)),
            pl.BlockSpec((width, D), lambda i: (k_off + i, 0)),
            pl.BlockSpec((width, D), lambda i: (v_off + i, 0)),
        ],
        out_specs=[
            pl.BlockSpec((rows, width), lambda i: (0, i)),
            pl.BlockSpec((rows, width), lambda i: (0, i)),
            pl.BlockSpec((heads_per_step, DH, DH), lambda i: (i, 0, 0)),
        ],
        out_shape=[
            jax.ShapeDtypeStruct((rows, D), jnp.bfloat16),
            jax.ShapeDtypeStruct((rows, D), jnp.bfloat16),
            jax.ShapeDtypeStruct((H, DH, DH), jnp.bfloat16),
        ],
    )(normed, weight_t, weight_t)


def tail_kernel(m_ref, q_ref, w_ref, gain_ref, o_ref):
    for j in range(m_ref.shape[0]):
        carried = jnp.dot(q_ref[j], m_ref[j].astype(jnp.bfloat16), preferred_element_type=jnp.float32)
        numerator = carried + w_ref[j]
        scale = lax.rsqrt(jnp.mean(numerator * numerator, axis=-1, keepdims=True) + epsilon)
        part = slice(j * DH, (j + 1) * DH)
        o_ref[:, part] = (numerator * scale * gain_ref[:, part]).astype(o_ref.dtype)


def attend_tail(memory, queries, within, gains, heads_per_step=4):
    rows = queries.shape[1]
    width = heads_per_step * DH
    return pl.pallas_call(
        tail_kernel,
        grid=(H // heads_per_step,),
        in_specs=[
            pl.BlockSpec((heads_per_step, DH, DH), lambda i: (i, 0, 0)),
            pl.BlockSpec((heads_per_step, rows, DH), lambda i: (i, 0, 0)),
            pl.BlockSpec((heads_per_step, rows, DH), lambda i: (i, 0, 0)),
            pl.BlockSpec((1, width), lambda i: (0, i)),
        ],
        out_specs=pl.BlockSpec((rows, width), lambda i: (0, i)),
        out_shape=jax.ShapeDtypeStruct((rows, H * DH), jnp.bfloat16),
    )(memory, queries, within, gains)


def ring_shift(value, axis, shift, size, wrap=True):
    pairs = [(j, (j + shift) % size) for j in range(size) if wrap or j + shift < size]
    return lax.ppermute(value, axis, pairs)


def memory_before(local):
    n_x = lax.axis_size("x")
    n_y = lax.axis_size("y")
    x_here = lax.axis_index("x")
    half = local.shape[0] // 2
    from_left = ring_shift(local, "x", 1, n_x)
    from_right = ring_shift(local, "x", -1, n_x)
    far = jnp.concatenate(
        [ring_shift(from_left[:half], "x", 1, n_x), ring_shift(from_right[half:], "x", -1, n_x)], axis=0
    )
    f32 = lambda v: v.astype(jnp.float32)
    row_total = f32(local) + f32(from_left) + f32(far) + f32(from_right)
    row_before = (
        jnp.where(x_here >= 1, f32(from_left), 0.0)
        + jnp.where(x_here >= 2, f32(far), 0.0)
        + jnp.where(x_here >= 3, f32(from_right), 0.0)
    )
    per = local.shape[0] // n_x
    quarter = lax.dynamic_slice_in_dim(row_total, x_here * per, per, axis=0)
    rows_before = quarter * 0.0
    for shift in range(1, n_y):
        rows_before = rows_before + ring_shift(quarter, "y", shift, n_y, wrap=False)
    got = [rows_before] + [ring_shift(rows_before, "x", k, n_x) for k in range(1, n_x)]
    stacked = jnp.stack(got)
    order = (x_here - jnp.arange(n_x)) % n_x
    earlier_rows = jnp.take(stacked, order, axis=0).reshape(local.shape)
    return earlier_rows + row_before


def body(tokens, input_gain, qkv_weight, head_gain, prefix_state):
    inputs = tokens[0].astype(jnp.float32)
    normed = inputs * lax.rsqrt(jnp.mean(inputs * inputs, axis=-1, keepdims=True) + epsilon)
    normed = (normed * input_gain.astype(jnp.float32)).astype(jnp.bfloat16)
    tok_rows = normed.shape[0]
    weight = lax.all_gather(qkv_weight, ("dp", "y", "x"), axis=1, tiled=True)
    key_feats, values, local = kv_memory(normed, weight.T)
    key_feats = key_feats.reshape(tok_rows, H, DH)
    values = values.reshape(tok_rows, H, DH)
    memory = prefix_state[0] + memory_before(local)
    queries = jnp.dot(normed, weight[:, :D], preferred_element_type=jnp.float32)
    queries = feature_map(queries).astype(jnp.bfloat16)

    causal = jnp.arange(tok_rows)[:, None] >= jnp.arange(tok_rows)[None, :]
    scores = jnp.einsum(
        "bhd,chd->hbc", queries.reshape(tok_rows, H, DH), key_feats, preferred_element_type=jnp.float32
    )
    scores = jnp.where(causal[None], scores, 0.0).astype(jnp.bfloat16)
    within = jnp.einsum("hbc,che->hbe", scores, values, preferred_element_type=jnp.float32)
    gains = head_gain.astype(jnp.float32).reshape(1, H * DH)
    attended = attend_tail(
        memory, jnp.transpose(queries.reshape(tok_rows, H, DH), (1, 0, 2)), within, gains
    )
    return attended.reshape(1, tok_rows, H * DH)


def solution(mesh):
    n_dp, n_seq = mesh.devices.shape
    n_x = int(round(n_seq ** 0.5))
    split = Mesh(mesh.devices.reshape(n_dp, n_seq // n_x, n_x), ("dp", "y", "x"))
    cols = ("y", "x")
    placed = (P("dp", cols, None), P(), P(None, ("dp", "y", "x")), P(), P("dp", None, None, None))
    return jax.shard_map(
        body, mesh=split, in_specs=placed, out_specs=P("dp", cols, None), check_vma=False
    )
```

```python
import jax
import jax.numpy as jnp
from jax import lax
from jax.experimental import pallas as pl
from jax.sharding import Mesh, PartitionSpec as P

D = 2048
H = 16
DH = 128
BLOCK = 512


epsilon = 1e-05


def feature_map(inputs):
    return jnp.where(inputs > 0, inputs + 1.0, jnp.exp(jnp.minimum(inputs, 0.0)))


def kv_memory_kernel(x_ref, wk_ref, wv_ref, k_ref, v_ref, m_ref):
    x = x_ref[...]
    dims = (((1,), (1,)), ((), ()))
    k = lax.dot_general(x, wk_ref[...], dims, preferred_element_type=jnp.float32)
    k = feature_map(k).astype(jnp.bfloat16)
    v = lax.dot_general(x, wv_ref[...], dims, preferred_element_type=jnp.float32).astype(jnp.bfloat16)
    k_ref[...] = k
    v_ref[...] = v
    for j in range(m_ref.shape[0]):
        part = slice(j * DH, (j + 1) * DH)
        m = lax.dot_general(k[:, part], v[:, part], (((0,), (0,)), ((), ())), preferred_element_type=jnp.float32)
        m_ref[j] = m.astype(jnp.bfloat16)


def kv_memory(normed, weight_t, heads_per_step=2):
    rows = normed.shape[0]
    width = heads_per_step * DH
    k_off = D // width
    v_off = 2 * D // width
    return pl.pallas_call(
        kv_memory_kernel,
        grid=(H // heads_per_step,),
        in_specs=[
            pl.BlockSpec((rows, D), lambda i: (0, 0)),
            pl.BlockSpec((width, D), lambda i: (k_off + i, 0)),
            pl.BlockSpec((width, D), lambda i: (v_off + i, 0)),
        ],
        out_specs=[
            pl.BlockSpec((rows, width), lambda i: (0, i)),
            pl.BlockSpec((rows, width), lambda i: (0, i)),
            pl.BlockSpec((heads_per_step, DH, DH), lambda i: (i, 0, 0)),
        ],
        out_shape=[
            jax.ShapeDtypeStruct((rows, D), jnp.bfloat16),
            jax.ShapeDtypeStruct((rows, D), jnp.bfloat16),
            jax.ShapeDtypeStruct((H, DH, DH), jnp.bfloat16),
        ],
    )(normed, weight_t, weight_t)


def tail_kernel(m_ref, q_ref, w_ref, gain_ref, o_ref):
    for j in range(m_ref.shape[0]):
        carried = jnp.dot(q_ref[j], m_ref[j].astype(jnp.bfloat16), preferred_element_type=jnp.float32)
        numerator = carried + w_ref[j]
        scale = lax.rsqrt(jnp.mean(numerator * numerator, axis=-1, keepdims=True) + epsilon)
        part = slice(j * DH, (j + 1) * DH)
        o_ref[:, part] = (numerator * scale * gain_ref[:, part]).astype(o_ref.dtype)


def attend_tail(memory, queries, within, gains, heads_per_step=4):
    rows = queries.shape[1]
    width = heads_per_step * DH
    return pl.pallas_call(
        tail_kernel,
        grid=(H // heads_per_step,),
        in_specs=[
            pl.BlockSpec((heads_per_step, DH, DH), lambda i: (i, 0, 0)),
            pl.BlockSpec((heads_per_step, rows, DH), lambda i: (i, 0, 0)),
            pl.BlockSpec((heads_per_step, rows, DH), lambda i: (i, 0, 0)),
            pl.BlockSpec((1, width), lambda i: (0, i)),
        ],
        out_specs=pl.BlockSpec((rows, width), lambda i: (0, i)),
        out_shape=jax.ShapeDtypeStruct((rows, H * DH), jnp.bfloat16),
    )(memory, queries, within, gains)


def ring_shift(value, axis, shift, size, wrap=True):
    pairs = [(j, (j + shift) % size) for j in range(size) if wrap or j + shift < size]
    return lax.ppermute(value, axis, pairs)


def memory_before(local, filler):
    n_x = lax.axis_size("x")
    n_y = lax.axis_size("y")
    x_here = lax.axis_index("x")
    half = local.shape[0] // 2
    from_left = ring_shift(local, "x", 1, n_x)
    from_right = ring_shift(local, "x", -1, n_x)
    far = jnp.concatenate(
        [ring_shift(from_left[:half], "x", 1, n_x), ring_shift(from_right[half:], "x", -1, n_x)], axis=0
    )
    f32 = lambda v: v.astype(jnp.float32)
    row_total = f32(local) + f32(from_left) + f32(far) + f32(from_right)
    row_before = (
        jnp.where(x_here >= 1, f32(from_left), 0.0)
        + jnp.where(x_here >= 2, f32(far), 0.0)
        + jnp.where(x_here >= 3, f32(from_right), 0.0)
    )
    per = local.shape[0] // n_x
    quarter = lax.dynamic_slice_in_dim(row_total, x_here * per, per, axis=0)
    quarter, filler = lax.optimization_barrier((quarter, filler))
    rows_before = quarter * 0.0
    for shift in range(1, n_y):
        rows_before = rows_before + ring_shift(quarter, "y", shift, n_y, wrap=False)
    got = [rows_before] + [ring_shift(rows_before, "x", k, n_x) for k in range(1, n_x)]
    stacked = jnp.stack(got)
    order = (x_here - jnp.arange(n_x)) % n_x
    earlier_rows = jnp.take(stacked, order, axis=0).reshape(local.shape)
    return earlier_rows + row_before, filler


def body(tokens, input_gain, qkv_weight, head_gain, prefix_state):
    inputs = tokens[0].astype(jnp.float32)
    normed = inputs * lax.rsqrt(jnp.mean(inputs * inputs, axis=-1, keepdims=True) + epsilon)
    normed = (normed * input_gain.astype(jnp.float32)).astype(jnp.bfloat16)
    tok_rows = normed.shape[0]
    weight = lax.all_gather(qkv_weight, ("dp", "y", "x"), axis=1, tiled=True)
    key_feats, values, local = kv_memory(normed, weight.T)
    key_feats = key_feats.reshape(tok_rows, H, DH)
    values = values.reshape(tok_rows, H, DH)
    queries = jnp.dot(normed, weight[:, :D], preferred_element_type=jnp.float32)
    queries = feature_map(queries).astype(jnp.bfloat16)

    causal = jnp.arange(tok_rows)[:, None] >= jnp.arange(tok_rows)[None, :]
    scores = jnp.einsum(
        "bhd,chd->hbc", queries.reshape(tok_rows, H, DH), key_feats, preferred_element_type=jnp.float32
    )
    scores = jnp.where(causal[None], scores, 0.0).astype(jnp.bfloat16)
    within = jnp.einsum("hbc,che->hbe", scores, values, preferred_element_type=jnp.float32)
    before, within = memory_before(local, within)
    memory = prefix_state[0] + before
    gains = head_gain.astype(jnp.float32).reshape(1, H * DH)
    attended = attend_tail(
        memory, jnp.transpose(queries.reshape(tok_rows, H, DH), (1, 0, 2)), within, gains
    )
    return attended.reshape(1, tok_rows, H * DH)


def solution(mesh):
    n_dp, n_seq = mesh.devices.shape
    n_x = int(round(n_seq ** 0.5))
    split = Mesh(mesh.devices.reshape(n_dp, n_seq // n_x, n_x), ("dp", "y", "x"))
    cols = ("y", "x")
    placed = (P("dp", cols, None), P(), P(None, ("dp", "y", "x")), P(), P("dp", None, None, None))
    return jax.shard_map(
        body, mesh=split, in_specs=placed, out_specs=P("dp", cols, None), check_vma=False
    )
```

```python
import jax
import jax.numpy as jnp
from jax import lax
from jax.experimental import pallas as pl
from jax.experimental.pallas import tpu as pltpu
from jax.sharding import Mesh, PartitionSpec as P

D = 2048
H = 16
DH = 128
BLOCK = 512


epsilon = 1e-05


def feature_map(inputs):
    return jnp.where(inputs > 0, inputs + 1.0, jnp.exp(jnp.minimum(inputs, 0.0)))


def kv_memory_kernel(x_ref, wk_ref, wv_ref, k_ref, v_ref, m_ref):
    x = x_ref[...]
    dims = (((1,), (1,)), ((), ()))
    k = lax.dot_general(x, wk_ref[...], dims, preferred_element_type=jnp.float32)
    k = feature_map(k).astype(jnp.bfloat16)
    v = lax.dot_general(x, wv_ref[...], dims, preferred_element_type=jnp.float32).astype(jnp.bfloat16)
    k_ref[...] = k
    v_ref[...] = v
    for j in range(m_ref.shape[0]):
        part = slice(j * DH, (j + 1) * DH)
        m = lax.dot_general(k[:, part], v[:, part], (((0,), (0,)), ((), ())), preferred_element_type=jnp.float32)
        m_ref[j] = m.astype(jnp.bfloat16)


def kv_memory(normed, weight_t, heads_per_step=4):
    rows = normed.shape[0]
    width = heads_per_step * DH
    k_off = D // width
    v_off = 2 * D // width
    return pl.pallas_call(
        kv_memory_kernel,
        grid=(H // heads_per_step,),
        in_specs=[
            pl.BlockSpec((rows, D), lambda i: (0, 0)),
            pl.BlockSpec((width, D), lambda i: (k_off + i, 0)),
            pl.BlockSpec((width, D), lambda i: (v_off + i, 0)),
        ],
        out_specs=[
            pl.BlockSpec((rows, width), lambda i: (0, i)),
            pl.BlockSpec((rows, width), lambda i: (0, i)),
            pl.BlockSpec((heads_per_step, DH, DH), lambda i: (i, 0, 0)),
        ],
        out_shape=[
            jax.ShapeDtypeStruct((rows, D), jnp.bfloat16),
            jax.ShapeDtypeStruct((rows, D), jnp.bfloat16),
            jax.ShapeDtypeStruct((H, DH, DH), jnp.bfloat16),
        ],
    )(normed, weight_t, weight_t)


def tail_kernel(here_ref, g_ref, p_ref, q_ref, w_ref, gain_ref, o_ref):
    here = here_ref[0]
    for j in range(p_ref.shape[0]):
        state = p_ref[j]
        for c in range(g_ref.shape[0]):
            state = state + jnp.where(c < here, g_ref[c, j].astype(jnp.float32), 0.0)
        carried = jnp.dot(q_ref[j], state.astype(jnp.bfloat16), preferred_element_type=jnp.float32)
        numerator = carried + w_ref[j]
        scale = lax.rsqrt(jnp.mean(numerator * numerator, axis=-1, keepdims=True) + epsilon)
        part = slice(j * DH, (j + 1) * DH)
        o_ref[:, part] = (numerator * scale * gain_ref[:, part]).astype(o_ref.dtype)


def attend_tail(here, gathered, prefix, queries, within, gains, heads_per_step=4):
    rows = queries.shape[1]
    n_piece = gathered.shape[0]
    width = heads_per_step * DH
    grid_spec = pltpu.PrefetchScalarGridSpec(
        num_scalar_prefetch=1,
        grid=(H // heads_per_step,),
        in_specs=[
            pl.BlockSpec((n_piece, heads_per_step, DH, DH), lambda i, s: (0, i, 0, 0)),
            pl.BlockSpec((heads_per_step, DH, DH), lambda i, s: (i, 0, 0)),
            pl.BlockSpec((heads_per_step, rows, DH), lambda i, s: (i, 0, 0)),
            pl.BlockSpec((heads_per_step, rows, DH), lambda i, s: (i, 0, 0)),
            pl.BlockSpec((1, width), lambda i, s: (0, i)),
        ],
        out_specs=pl.BlockSpec((rows, width), lambda i, s: (0, i)),
    )
    return pl.pallas_call(
        tail_kernel,
        grid_spec=grid_spec,
        out_shape=jax.ShapeDtypeStruct((rows, H * DH), jnp.bfloat16),
    )(here, gathered, prefix, queries, within, gains)


def body(tokens, input_gain, qkv_weight, head_gain, prefix_state):
    inputs = tokens[0].astype(jnp.float32)
    normed = inputs * lax.rsqrt(jnp.mean(inputs * inputs, axis=-1, keepdims=True) + epsilon)
    normed = (normed * input_gain.astype(jnp.float32)).astype(jnp.bfloat16)
    tok_rows = normed.shape[0]
    weight = lax.all_gather(qkv_weight, ("dp", "y", "x"), axis=1, tiled=True)
    key_feats, values, local = kv_memory(normed, weight.T)
    key_feats = key_feats.reshape(tok_rows, H, DH)
    values = values.reshape(tok_rows, H, DH)
    gathered = lax.all_gather(local[None], ("y", "x"), axis=0, tiled=True)
    seq_here = lax.axis_index(("y", "x")).astype(jnp.int32).reshape(1)
    queries = jnp.dot(normed, weight[:, :D], preferred_element_type=jnp.float32)
    queries = feature_map(queries).astype(jnp.bfloat16)

    causal = jnp.arange(tok_rows)[:, None] >= jnp.arange(tok_rows)[None, :]
    scores = jnp.einsum(
        "bhd,chd->hbc", queries.reshape(tok_rows, H, DH), key_feats, preferred_element_type=jnp.float32
    )
    scores = jnp.where(causal[None], scores, 0.0).astype(jnp.bfloat16)
    within = jnp.einsum("hbc,che->hbe", scores, values, preferred_element_type=jnp.float32)
    gains = head_gain.astype(jnp.float32).reshape(1, H * DH)
    attended = attend_tail(
        seq_here, gathered, prefix_state[0], jnp.transpose(queries.reshape(tok_rows, H, DH), (1, 0, 2)), within, gains
    )
    return attended.reshape(1, tok_rows, H * DH)


def solution(mesh):
    n_dp, n_seq = mesh.devices.shape
    n_x = int(round(n_seq ** 0.5))
    split = Mesh(mesh.devices.reshape(n_dp, n_seq // n_x, n_x), ("dp", "y", "x"))
    cols = ("y", "x")
    placed = (P("dp", cols, None), P(), P(None, ("dp", "y", "x")), P(), P("dp", None, None, None))
    return jax.shard_map(
        body, mesh=split, in_specs=placed, out_specs=P("dp", cols, None), check_vma=False
    )
```

```python
import jax
import jax.numpy as jnp
from jax import lax
from jax.experimental import pallas as pl
from jax.sharding import Mesh, PartitionSpec as P

D = 2048
H = 16
DH = 128
BLOCK = 512


epsilon = 1e-05


def feature_map(inputs):
    return jnp.where(inputs > 0, inputs + 1.0, jnp.exp(jnp.minimum(inputs, 0.0)))


def kv_memory_kernel(x_ref, wk_ref, wv_ref, k_ref, v_ref, m_ref):
    x = x_ref[...]
    dims = (((1,), (1,)), ((), ()))
    k = lax.dot_general(x, wk_ref[...], dims, preferred_element_type=jnp.float32)
    k = feature_map(k).astype(jnp.bfloat16)
    v = lax.dot_general(x, wv_ref[...], dims, preferred_element_type=jnp.float32).astype(jnp.bfloat16)
    k_ref[...] = k
    v_ref[...] = v
    for j in range(m_ref.shape[0]):
        part = slice(j * DH, (j + 1) * DH)
        m = lax.dot_general(k[:, part], v[:, part], (((0,), (0,)), ((), ())), preferred_element_type=jnp.float32)
        m_ref[j] = m.astype(jnp.bfloat16)


def kv_memory(normed, weight_t, heads_per_step=4):
    rows = normed.shape[0]
    width = heads_per_step * DH
    k_off = D // width
    v_off = 2 * D // width
    return pl.pallas_call(
        kv_memory_kernel,
        grid=(H // heads_per_step,),
        in_specs=[
            pl.BlockSpec((rows, D), lambda i: (0, 0)),
            pl.BlockSpec((width, D), lambda i: (k_off + i, 0)),
            pl.BlockSpec((width, D), lambda i: (v_off + i, 0)),
        ],
        out_specs=[
            pl.BlockSpec((rows, width), lambda i: (0, i)),
            pl.BlockSpec((rows, width), lambda i: (0, i)),
            pl.BlockSpec((heads_per_step, DH, DH), lambda i: (i, 0, 0)),
        ],
        out_shape=[
            jax.ShapeDtypeStruct((rows, D), jnp.bfloat16),
            jax.ShapeDtypeStruct((rows, D), jnp.bfloat16),
            jax.ShapeDtypeStruct((H, DH, DH), jnp.bfloat16),
        ],
    )(normed, weight_t, weight_t)


def tail_kernel(m_ref, q_ref, w_ref, gain_ref, o_ref):
    for j in range(m_ref.shape[0]):
        carried = jnp.dot(q_ref[j], m_ref[j].astype(jnp.bfloat16), preferred_element_type=jnp.float32)
        numerator = carried + w_ref[j]
        scale = lax.rsqrt(jnp.mean(numerator * numerator, axis=-1, keepdims=True) + epsilon)
        part = slice(j * DH, (j + 1) * DH)
        o_ref[:, part] = (numerator * scale * gain_ref[:, part]).astype(o_ref.dtype)


def attend_tail(memory, queries, within, gains, heads_per_step=4):
    rows = queries.shape[1]
    width = heads_per_step * DH
    return pl.pallas_call(
        tail_kernel,
        grid=(H // heads_per_step,),
        in_specs=[
            pl.BlockSpec((heads_per_step, DH, DH), lambda i: (i, 0, 0)),
            pl.BlockSpec((heads_per_step, rows, DH), lambda i: (i, 0, 0)),
            pl.BlockSpec((heads_per_step, rows, DH), lambda i: (i, 0, 0)),
            pl.BlockSpec((1, width), lambda i: (0, i)),
        ],
        out_specs=pl.BlockSpec((rows, width), lambda i: (0, i)),
        out_shape=jax.ShapeDtypeStruct((rows, H * DH), jnp.bfloat16),
    )(memory, queries, within, gains)


def ring_shift(value, axis, shift, size, wrap=True):
    pairs = [(j, (j + shift) % size) for j in range(size) if wrap or j + shift < size]
    return lax.ppermute(value, axis, pairs)


def memory_before(local, filler):
    n_x = lax.axis_size("x")
    n_y = lax.axis_size("y")
    x_here = lax.axis_index("x")
    half = local.shape[0] // 2
    from_left = ring_shift(local, "x", 1, n_x)
    from_right = ring_shift(local, "x", -1, n_x)
    far = jnp.concatenate(
        [ring_shift(from_left[:half], "x", 1, n_x), ring_shift(from_right[half:], "x", -1, n_x)], axis=0
    )
    f32 = lambda v: v.astype(jnp.float32)
    row_total = f32(local) + f32(from_left) + f32(far) + f32(from_right)
    row_before = (
        jnp.where(x_here >= 1, f32(from_left), 0.0)
        + jnp.where(x_here >= 2, f32(far), 0.0)
        + jnp.where(x_here >= 3, f32(from_right), 0.0)
    )
    per = local.shape[0] // n_x
    quarter = lax.dynamic_slice_in_dim(row_total, x_here * per, per, axis=0)
    quarter, filler = lax.optimization_barrier((quarter, filler))
    rows_before = quarter * 0.0
    for shift in range(1, n_y):
        rows_before = rows_before + ring_shift(quarter, "y", shift, n_y, wrap=False)
    got = [rows_before] + [ring_shift(rows_before, "x", k, n_x) for k in range(1, n_x)]
    stacked = jnp.stack(got)
    order = (x_here - jnp.arange(n_x)) % n_x
    earlier_rows = jnp.take(stacked, order, axis=0).reshape(local.shape)
    return earlier_rows + row_before, filler


def body(tokens, input_gain, qkv_weight, head_gain, prefix_state):
    inputs = tokens[0].astype(jnp.float32)
    normed = inputs * lax.rsqrt(jnp.mean(inputs * inputs, axis=-1, keepdims=True) + epsilon)
    normed = (normed * input_gain.astype(jnp.float32)).astype(jnp.bfloat16)
    tok_rows = normed.shape[0]
    weight = lax.all_gather(qkv_weight, ("dp", "y", "x"), axis=1, tiled=True)
    key_feats, values, local = kv_memory(normed, weight.T)
    key_feats = key_feats.reshape(tok_rows, H, DH)
    values = values.reshape(tok_rows, H, DH)
    half = H // 2
    gathered = lax.all_gather(local[None, :half], ("y", "x"), axis=0, tiled=True)
    queries = jnp.dot(normed, weight[:, :D], preferred_element_type=jnp.float32)
    queries = feature_map(queries).astype(jnp.bfloat16)

    causal = jnp.arange(tok_rows)[:, None] >= jnp.arange(tok_rows)[None, :]
    scores = jnp.einsum(
        "bhd,chd->hbc", queries.reshape(tok_rows, H, DH), key_feats, preferred_element_type=jnp.float32
    )
    scores = jnp.where(causal[None], scores, 0.0).astype(jnp.bfloat16)
    within = jnp.einsum("hbc,che->hbe", scores, values, preferred_element_type=jnp.float32)
    before_late, within = memory_before(local[half:], within)
    seq_here = lax.axis_index(("y", "x"))
    earlier = (jnp.arange(gathered.shape[0]) < seq_here)[:, None, None, None]
    before_early = jnp.sum(jnp.where(earlier, gathered.astype(jnp.float32), 0.0), axis=0)
    memory = prefix_state[0] + jnp.concatenate([before_early, before_late], axis=0)
    gains = head_gain.astype(jnp.float32).reshape(1, H * DH)
    attended = attend_tail(
        memory, jnp.transpose(queries.reshape(tok_rows, H, DH), (1, 0, 2)), within, gains
    )
    return attended.reshape(1, tok_rows, H * DH)


def solution(mesh):
    n_dp, n_seq = mesh.devices.shape
    n_x = int(round(n_seq ** 0.5))
    split = Mesh(mesh.devices.reshape(n_dp, n_seq // n_x, n_x), ("dp", "y", "x"))
    cols = ("y", "x")
    placed = (P("dp", cols, None), P(), P(None, ("dp", "y", "x")), P(), P("dp", None, None, None))
    return jax.shard_map(
        body, mesh=split, in_specs=placed, out_specs=P("dp", cols, None), check_vma=False
    )
```

```python
import jax
import jax.numpy as jnp
from jax import lax
from jax.experimental import pallas as pl
from jax.experimental.pallas import tpu as pltpu
from jax.sharding import Mesh, PartitionSpec as P

D = 2048
H = 16
DH = 128
BLOCK = 512


epsilon = 1e-05


def feature_map(inputs):
    return jnp.where(inputs > 0, inputs + 1.0, jnp.exp(jnp.minimum(inputs, 0.0)))


def kv_memory_kernel(x_ref, wk_ref, wv_ref, k_ref, v_ref, m_ref):
    x = x_ref[...]
    dims = (((1,), (1,)), ((), ()))
    k = lax.dot_general(x, wk_ref[...], dims, preferred_element_type=jnp.float32)
    k = feature_map(k).astype(jnp.bfloat16)
    v = lax.dot_general(x, wv_ref[...], dims, preferred_element_type=jnp.float32).astype(jnp.bfloat16)
    k_ref[...] = k
    v_ref[...] = v
    for j in range(m_ref.shape[0]):
        part = slice(j * DH, (j + 1) * DH)
        m = lax.dot_general(k[:, part], v[:, part], (((0,), (0,)), ((), ())), preferred_element_type=jnp.float32)
        m_ref[j] = m.astype(jnp.bfloat16)


def kv_memory(normed, weight_t, heads_per_step=4):
    rows = normed.shape[0]
    width = heads_per_step * DH
    k_off = D // width
    v_off = 2 * D // width
    return pl.pallas_call(
        kv_memory_kernel,
        grid=(H // heads_per_step,),
        in_specs=[
            pl.BlockSpec((rows, D), lambda i: (0, 0)),
            pl.BlockSpec((width, D), lambda i: (k_off + i, 0)),
            pl.BlockSpec((width, D), lambda i: (v_off + i, 0)),
        ],
        out_specs=[
            pl.BlockSpec((rows, width), lambda i: (0, i)),
            pl.BlockSpec((rows, width), lambda i: (0, i)),
            pl.BlockSpec((heads_per_step, DH, DH), lambda i: (i, 0, 0)),
        ],
        out_shape=[
            jax.ShapeDtypeStruct((rows, D), jnp.bfloat16),
            jax.ShapeDtypeStruct((rows, D), jnp.bfloat16),
            jax.ShapeDtypeStruct((H, DH, DH), jnp.bfloat16),
        ],
    )(normed, weight_t, weight_t)


def tail_kernel(m_ref, q_ref, w_ref, gain_ref, o_ref):
    for j in range(m_ref.shape[0]):
        carried = jnp.dot(q_ref[j], m_ref[j].astype(jnp.bfloat16), preferred_element_type=jnp.float32)
        numerator = carried + w_ref[j]
        scale = lax.rsqrt(jnp.mean(numerator * numerator, axis=-1, keepdims=True) + epsilon)
        part = slice(j * DH, (j + 1) * DH)
        o_ref[:, part] = (numerator * scale * gain_ref[:, part]).astype(o_ref.dtype)


def attend_tail(memory, queries, within, gains, heads_per_step=4):
    rows = queries.shape[1]
    width = heads_per_step * DH
    return pl.pallas_call(
        tail_kernel,
        grid=(H // heads_per_step,),
        in_specs=[
            pl.BlockSpec((heads_per_step, DH, DH), lambda i: (i, 0, 0)),
            pl.BlockSpec((heads_per_step, rows, DH), lambda i: (i, 0, 0)),
            pl.BlockSpec((heads_per_step, rows, DH), lambda i: (i, 0, 0)),
            pl.BlockSpec((1, width), lambda i: (0, i)),
        ],
        out_specs=pl.BlockSpec((rows, width), lambda i: (0, i)),
        out_shape=jax.ShapeDtypeStruct((rows, H * DH), jnp.bfloat16),
    )(memory, queries, within, gains)


def tail_gathered_kernel(here_ref, g_ref, p_ref, q_ref, w_ref, gain_ref, o_ref):
    here = here_ref[0]
    for j in range(p_ref.shape[0]):
        state = p_ref[j]
        for c in range(g_ref.shape[0]):
            state = state + jnp.where(c < here, g_ref[c, j].astype(jnp.float32), 0.0)
        carried = jnp.dot(q_ref[j], state.astype(jnp.bfloat16), preferred_element_type=jnp.float32)
        numerator = carried + w_ref[j]
        scale = lax.rsqrt(jnp.mean(numerator * numerator, axis=-1, keepdims=True) + epsilon)
        part = slice(j * DH, (j + 1) * DH)
        o_ref[:, part] = (numerator * scale * gain_ref[:, part]).astype(o_ref.dtype)


def tail_from_memory_kernel(m_ref, q_ref, w_ref, gain_ref, prior_ref, o_ref):
    del prior_ref
    tail_kernel(m_ref, q_ref, w_ref, gain_ref, o_ref)


def attend_tail_split(here, gathered, prefix, late_memory, queries, within, gains, heads_per_step=4):
    rows = queries.shape[1]
    width = heads_per_step * DH
    n_piece = gathered.shape[0]
    early = gathered.shape[1] // heads_per_step
    late = late_memory.shape[0] // heads_per_step
    grid_spec = pltpu.PrefetchScalarGridSpec(
        num_scalar_prefetch=1,
        grid=(early,),
        in_specs=[
            pl.BlockSpec((n_piece, heads_per_step, DH, DH), lambda i, s: (0, i, 0, 0)),
            pl.BlockSpec((heads_per_step, DH, DH), lambda i, s: (i, 0, 0)),
            pl.BlockSpec((heads_per_step, rows, DH), lambda i, s: (i, 0, 0)),
            pl.BlockSpec((heads_per_step, rows, DH), lambda i, s: (i, 0, 0)),
            pl.BlockSpec((1, width), lambda i, s: (0, i)),
        ],
        out_specs=pl.BlockSpec((rows, width), lambda i, s: (0, i)),
    )
    first = pl.pallas_call(
        tail_gathered_kernel,
        grid_spec=grid_spec,
        out_shape=jax.ShapeDtypeStruct((rows, H * DH), jnp.bfloat16),
    )(here, gathered, prefix, queries, within, gains)
    return pl.pallas_call(
        tail_from_memory_kernel,
        grid=(late,),
        in_specs=[
            pl.BlockSpec((heads_per_step, DH, DH), lambda i: (i, 0, 0)),
            pl.BlockSpec((heads_per_step, rows, DH), lambda i: (early + i, 0, 0)),
            pl.BlockSpec((heads_per_step, rows, DH), lambda i: (early + i, 0, 0)),
            pl.BlockSpec((1, width), lambda i: (0, early + i)),
            pl.BlockSpec(memory_space=pl.ANY),
        ],
        out_specs=pl.BlockSpec((rows, width), lambda i: (0, early + i)),
        out_shape=jax.ShapeDtypeStruct((rows, H * DH), jnp.bfloat16),
        input_output_aliases={4: 0},
    )(late_memory, queries, within, gains, first)


def ring_shift(value, axis, shift, size, wrap=True):
    pairs = [(j, (j + shift) % size) for j in range(size) if wrap or j + shift < size]
    return lax.ppermute(value, axis, pairs)


def memory_before(local, filler):
    n_x = lax.axis_size("x")
    n_y = lax.axis_size("y")
    x_here = lax.axis_index("x")
    half = local.shape[0] // 2
    from_left = ring_shift(local, "x", 1, n_x)
    from_right = ring_shift(local, "x", -1, n_x)
    far = jnp.concatenate(
        [ring_shift(from_left[:half], "x", 1, n_x), ring_shift(from_right[half:], "x", -1, n_x)], axis=0
    )
    f32 = lambda v: v.astype(jnp.float32)
    row_total = f32(local) + f32(from_left) + f32(far) + f32(from_right)
    row_before = (
        jnp.where(x_here >= 1, f32(from_left), 0.0)
        + jnp.where(x_here >= 2, f32(far), 0.0)
        + jnp.where(x_here >= 3, f32(from_right), 0.0)
    )
    per = local.shape[0] // n_x
    quarter = lax.dynamic_slice_in_dim(row_total, x_here * per, per, axis=0)
    quarter, filler = lax.optimization_barrier((quarter, filler))
    rows_before = quarter * 0.0
    for shift in range(1, n_y):
        rows_before = rows_before + ring_shift(quarter, "y", shift, n_y, wrap=False)
    got = [rows_before] + [ring_shift(rows_before, "x", k, n_x) for k in range(1, n_x)]
    stacked = jnp.stack(got)
    order = (x_here - jnp.arange(n_x)) % n_x
    earlier_rows = jnp.take(stacked, order, axis=0).reshape(local.shape)
    return earlier_rows + row_before, filler


def body(tokens, input_gain, qkv_weight, head_gain, prefix_state):
    inputs = tokens[0].astype(jnp.float32)
    normed = inputs * lax.rsqrt(jnp.mean(inputs * inputs, axis=-1, keepdims=True) + epsilon)
    normed = (normed * input_gain.astype(jnp.float32)).astype(jnp.bfloat16)
    tok_rows = normed.shape[0]
    weight = lax.all_gather(qkv_weight, ("dp", "y", "x"), axis=1, tiled=True)
    key_feats, values, local = kv_memory(normed, weight.T)
    key_feats = key_feats.reshape(tok_rows, H, DH)
    values = values.reshape(tok_rows, H, DH)
    half = H // 2
    gathered = lax.all_gather(local[None, :half], ("y", "x"), axis=0, tiled=True)
    queries = jnp.dot(normed, weight[:, :D], preferred_element_type=jnp.float32)
    queries = feature_map(queries).astype(jnp.bfloat16)

    causal = jnp.arange(tok_rows)[:, None] >= jnp.arange(tok_rows)[None, :]
    scores = jnp.einsum(
        "bhd,chd->hbc", queries.reshape(tok_rows, H, DH), key_feats, preferred_element_type=jnp.float32
    )
    scores = jnp.where(causal[None], scores, 0.0).astype(jnp.bfloat16)
    within = jnp.einsum("hbc,che->hbe", scores, values, preferred_element_type=jnp.float32)
    before_late, within = memory_before(local[half:], within)
    seq_here = lax.axis_index(("y", "x")).astype(jnp.int32).reshape(1)
    late_memory = prefix_state[0, half:] + before_late
    gains = head_gain.astype(jnp.float32).reshape(1, H * DH)
    attended = attend_tail_split(
        seq_here, gathered, prefix_state[0], late_memory,
        jnp.transpose(queries.reshape(tok_rows, H, DH), (1, 0, 2)), within, gains,
    )
    return attended.reshape(1, tok_rows, H * DH)


def solution(mesh):
    n_dp, n_seq = mesh.devices.shape
    n_x = int(round(n_seq ** 0.5))
    split = Mesh(mesh.devices.reshape(n_dp, n_seq // n_x, n_x), ("dp", "y", "x"))
    cols = ("y", "x")
    placed = (P("dp", cols, None), P(), P(None, ("dp", "y", "x")), P(), P("dp", None, None, None))
    return jax.shard_map(
        body, mesh=split, in_specs=placed, out_specs=P("dp", cols, None), check_vma=False
    )
```

```python
import jax
import jax.numpy as jnp
from jax import lax
from jax.experimental import pallas as pl
from jax.experimental.pallas import tpu as pltpu
from jax.sharding import Mesh, PartitionSpec as P

D = 2048
H = 16
DH = 128
BLOCK = 512


epsilon = 1e-05


def feature_map(inputs):
    return jnp.where(inputs > 0, inputs + 1.0, jnp.exp(jnp.minimum(inputs, 0.0)))


def kv_memory_kernel(x_ref, wk_ref, wv_ref, k_ref, v_ref, m_ref):
    x = x_ref[...]
    dims = (((1,), (1,)), ((), ()))
    k = lax.dot_general(x, wk_ref[...], dims, preferred_element_type=jnp.float32)
    k = feature_map(k).astype(jnp.bfloat16)
    v = lax.dot_general(x, wv_ref[...], dims, preferred_element_type=jnp.float32).astype(jnp.bfloat16)
    k_ref[...] = k
    v_ref[...] = v
    for j in range(m_ref.shape[0]):
        part = slice(j * DH, (j + 1) * DH)
        m = lax.dot_general(k[:, part], v[:, part], (((0,), (0,)), ((), ())), preferred_element_type=jnp.float32)
        m_ref[j] = m.astype(jnp.bfloat16)


def kv_memory(normed, weight_t, heads_per_step=4):
    rows = normed.shape[0]
    width = heads_per_step * DH
    k_off = D // width
    v_off = 2 * D // width
    return pl.pallas_call(
        kv_memory_kernel,
        grid=(H // heads_per_step,),
        in_specs=[
            pl.BlockSpec((rows, D), lambda i: (0, 0)),
            pl.BlockSpec((width, D), lambda i: (k_off + i, 0)),
            pl.BlockSpec((width, D), lambda i: (v_off + i, 0)),
        ],
        out_specs=[
            pl.BlockSpec((rows, width), lambda i: (0, i)),
            pl.BlockSpec((rows, width), lambda i: (0, i)),
            pl.BlockSpec((heads_per_step, DH, DH), lambda i: (i, 0, 0)),
        ],
        out_shape=[
            jax.ShapeDtypeStruct((rows, D), jnp.bfloat16),
            jax.ShapeDtypeStruct((rows, D), jnp.bfloat16),
            jax.ShapeDtypeStruct((H, DH, DH), jnp.bfloat16),
        ],
    )(normed, weight_t, weight_t)


def tail_kernel(m_ref, q_ref, w_ref, gain_ref, o_ref):
    for j in range(m_ref.shape[0]):
        carried = jnp.dot(q_ref[j], m_ref[j].astype(jnp.bfloat16), preferred_element_type=jnp.float32)
        numerator = carried + w_ref[j]
        scale = lax.rsqrt(jnp.mean(numerator * numerator, axis=-1, keepdims=True) + epsilon)
        part = slice(j * DH, (j + 1) * DH)
        o_ref[:, part] = (numerator * scale * gain_ref[:, part]).astype(o_ref.dtype)


def attend_tail(memory, queries, within, gains, heads_per_step=4):
    rows = queries.shape[1]
    width = heads_per_step * DH
    return pl.pallas_call(
        tail_kernel,
        grid=(H // heads_per_step,),
        in_specs=[
            pl.BlockSpec((heads_per_step, DH, DH), lambda i: (i, 0, 0)),
            pl.BlockSpec((heads_per_step, rows, DH), lambda i: (i, 0, 0)),
            pl.BlockSpec((heads_per_step, rows, DH), lambda i: (i, 0, 0)),
            pl.BlockSpec((1, width), lambda i: (0, i)),
        ],
        out_specs=pl.BlockSpec((rows, width), lambda i: (0, i)),
        out_shape=jax.ShapeDtypeStruct((rows, H * DH), jnp.bfloat16),
    )(memory, queries, within, gains)


def tail_gathered_kernel(here_ref, g_ref, p_ref, q_ref, w_ref, gain_ref, o_ref):
    here = here_ref[0]
    for j in range(p_ref.shape[0]):
        state = p_ref[j]
        for c in range(g_ref.shape[0]):
            state = state + jnp.where(c < here, g_ref[c, j].astype(jnp.float32), 0.0)
        carried = jnp.dot(q_ref[j], state.astype(jnp.bfloat16), preferred_element_type=jnp.float32)
        numerator = carried + w_ref[j]
        scale = lax.rsqrt(jnp.mean(numerator * numerator, axis=-1, keepdims=True) + epsilon)
        part = slice(j * DH, (j + 1) * DH)
        o_ref[:, part] = (numerator * scale * gain_ref[:, part]).astype(o_ref.dtype)


def tail_from_memory_kernel(m_ref, q_ref, w_ref, gain_ref, prior_ref, o_ref):
    del prior_ref
    tail_kernel(m_ref, q_ref, w_ref, gain_ref, o_ref)


def attend_tail_split(here, gathered, prefix, late_memory, queries, within, gains, heads_per_step=4):
    rows = queries.shape[1]
    width = heads_per_step * DH
    n_piece = gathered.shape[0]
    early = gathered.shape[1] // heads_per_step
    late = late_memory.shape[0] // heads_per_step
    grid_spec = pltpu.PrefetchScalarGridSpec(
        num_scalar_prefetch=1,
        grid=(early,),
        in_specs=[
            pl.BlockSpec((n_piece, heads_per_step, DH, DH), lambda i, s: (0, i, 0, 0)),
            pl.BlockSpec((heads_per_step, DH, DH), lambda i, s: (i, 0, 0)),
            pl.BlockSpec((heads_per_step, rows, DH), lambda i, s: (i, 0, 0)),
            pl.BlockSpec((heads_per_step, rows, DH), lambda i, s: (i, 0, 0)),
            pl.BlockSpec((1, width), lambda i, s: (0, i)),
        ],
        out_specs=pl.BlockSpec((rows, width), lambda i, s: (0, i)),
    )
    first = pl.pallas_call(
        tail_gathered_kernel,
        grid_spec=grid_spec,
        out_shape=jax.ShapeDtypeStruct((rows, H * DH), jnp.bfloat16),
    )(here, gathered, prefix, queries, within, gains)
    return pl.pallas_call(
        tail_from_memory_kernel,
        grid=(late,),
        in_specs=[
            pl.BlockSpec((heads_per_step, DH, DH), lambda i: (i, 0, 0)),
            pl.BlockSpec((heads_per_step, rows, DH), lambda i: (early + i, 0, 0)),
            pl.BlockSpec((heads_per_step, rows, DH), lambda i: (early + i, 0, 0)),
            pl.BlockSpec((1, width), lambda i: (0, early + i)),
            pl.BlockSpec(memory_space=pl.ANY),
        ],
        out_specs=pl.BlockSpec((rows, width), lambda i: (0, early + i)),
        out_shape=jax.ShapeDtypeStruct((rows, H * DH), jnp.bfloat16),
        input_output_aliases={4: 0},
    )(late_memory, queries, within, gains, first)


def ring_shift(value, axis, shift, size, wrap=True):
    pairs = [(j, (j + shift) % size) for j in range(size) if wrap or j + shift < size]
    return lax.ppermute(value, axis, pairs)


def memory_before(local, filler):
    n_x = lax.axis_size("x")
    n_y = lax.axis_size("y")
    x_here = lax.axis_index("x")
    half = local.shape[0] // 2
    from_left = ring_shift(local, "x", 1, n_x)
    from_right = ring_shift(local, "x", -1, n_x)
    far = jnp.concatenate(
        [ring_shift(from_left[:half], "x", 1, n_x), ring_shift(from_right[half:], "x", -1, n_x)], axis=0
    )
    f32 = lambda v: v.astype(jnp.float32)
    row_total = f32(local) + f32(from_left) + f32(far) + f32(from_right)
    row_before = (
        jnp.where(x_here >= 1, f32(from_left), 0.0)
        + jnp.where(x_here >= 2, f32(far), 0.0)
        + jnp.where(x_here >= 3, f32(from_right), 0.0)
    )
    row_total, filler = lax.optimization_barrier((row_total, filler))
    earlier_rows = row_total * 0.0
    for shift in range(1, n_y):
        earlier_rows = earlier_rows + ring_shift(row_total, "y", shift, n_y, wrap=False)
    return earlier_rows + row_before, filler


def body(tokens, input_gain, qkv_weight, head_gain, prefix_state):
    inputs = tokens[0].astype(jnp.float32)
    normed = inputs * lax.rsqrt(jnp.mean(inputs * inputs, axis=-1, keepdims=True) + epsilon)
    normed = (normed * input_gain.astype(jnp.float32)).astype(jnp.bfloat16)
    tok_rows = normed.shape[0]
    weight = lax.all_gather(qkv_weight, ("dp", "y", "x"), axis=1, tiled=True)
    key_feats, values, local = kv_memory(normed, weight.T)
    key_feats = key_feats.reshape(tok_rows, H, DH)
    values = values.reshape(tok_rows, H, DH)
    half = H // 2
    gathered = lax.all_gather(local[None, :half], ("y", "x"), axis=0, tiled=True)
    queries = jnp.dot(normed, weight[:, :D], preferred_element_type=jnp.float32)
    queries = feature_map(queries).astype(jnp.bfloat16)

    causal = jnp.arange(tok_rows)[:, None] >= jnp.arange(tok_rows)[None, :]
    scores = jnp.einsum(
        "bhd,chd->hbc", queries.reshape(tok_rows, H, DH), key_feats, preferred_element_type=jnp.float32
    )
    scores = jnp.where(causal[None], scores, 0.0).astype(jnp.bfloat16)
    within = jnp.einsum("hbc,che->hbe", scores, values, preferred_element_type=jnp.float32)
    before_late, within = memory_before(local[half:], within)
    seq_here = lax.axis_index(("y", "x")).astype(jnp.int32).reshape(1)
    late_memory = prefix_state[0, half:] + before_late
    gains = head_gain.astype(jnp.float32).reshape(1, H * DH)
    attended = attend_tail_split(
        seq_here, gathered, prefix_state[0], late_memory,
        jnp.transpose(queries.reshape(tok_rows, H, DH), (1, 0, 2)), within, gains,
    )
    return attended.reshape(1, tok_rows, H * DH)


def solution(mesh):
    n_dp, n_seq = mesh.devices.shape
    n_x = int(round(n_seq ** 0.5))
    split = Mesh(mesh.devices.reshape(n_dp, n_seq // n_x, n_x), ("dp", "y", "x"))
    cols = ("y", "x")
    placed = (P("dp", cols, None), P(), P(None, ("dp", "y", "x")), P(), P("dp", None, None, None))
    return jax.shard_map(
        body, mesh=split, in_specs=placed, out_specs=P("dp", cols, None), check_vma=False
    )
```

```python
import jax
import jax.numpy as jnp
from jax import lax
from jax.experimental import pallas as pl
from jax.experimental.pallas import tpu as pltpu
from jax.sharding import Mesh, PartitionSpec as P

D = 2048
H = 16
DH = 128
BLOCK = 512


epsilon = 1e-05


def feature_map(inputs):
    return jnp.where(inputs > 0, inputs + 1.0, jnp.exp(jnp.minimum(inputs, 0.0)))


def kv_memory_kernel(x_ref, wk_ref, wv_ref, k_ref, v_ref, m_ref):
    x = x_ref[...]
    dims = (((1,), (1,)), ((), ()))
    k = lax.dot_general(x, wk_ref[...], dims, preferred_element_type=jnp.float32)
    k = feature_map(k).astype(jnp.bfloat16)
    v = lax.dot_general(x, wv_ref[...], dims, preferred_element_type=jnp.float32).astype(jnp.bfloat16)
    k_ref[...] = k
    v_ref[...] = v
    for j in range(m_ref.shape[0]):
        part = slice(j * DH, (j + 1) * DH)
        m = lax.dot_general(k[:, part], v[:, part], (((0,), (0,)), ((), ())), preferred_element_type=jnp.float32)
        m_ref[j] = m.astype(jnp.bfloat16)


def kv_memory(normed, weight_t, first_head, n_heads, heads_per_step=4):
    rows = normed.shape[0]
    width = heads_per_step * DH
    k_off = (D + first_head * DH) // width
    v_off = (2 * D + first_head * DH) // width
    return pl.pallas_call(
        kv_memory_kernel,
        grid=(n_heads // heads_per_step,),
        in_specs=[
            pl.BlockSpec((rows, D), lambda i: (0, 0)),
            pl.BlockSpec((width, D), lambda i: (k_off + i, 0)),
            pl.BlockSpec((width, D), lambda i: (v_off + i, 0)),
        ],
        out_specs=[
            pl.BlockSpec((rows, width), lambda i: (0, i)),
            pl.BlockSpec((rows, width), lambda i: (0, i)),
            pl.BlockSpec((heads_per_step, DH, DH), lambda i: (i, 0, 0)),
        ],
        out_shape=[
            jax.ShapeDtypeStruct((rows, n_heads * DH), jnp.bfloat16),
            jax.ShapeDtypeStruct((rows, n_heads * DH), jnp.bfloat16),
            jax.ShapeDtypeStruct((n_heads, DH, DH), jnp.bfloat16),
        ],
    )(normed, weight_t, weight_t)


def tail_kernel(m_ref, q_ref, w_ref, gain_ref, o_ref):
    for j in range(m_ref.shape[0]):
        carried = jnp.dot(q_ref[j], m_ref[j].astype(jnp.bfloat16), preferred_element_type=jnp.float32)
        numerator = carried + w_ref[j]
        scale = lax.rsqrt(jnp.mean(numerator * numerator, axis=-1, keepdims=True) + epsilon)
        part = slice(j * DH, (j + 1) * DH)
        o_ref[:, part] = (numerator * scale * gain_ref[:, part]).astype(o_ref.dtype)


def attend_tail(memory, queries, within, gains, heads_per_step=4):
    rows = queries.shape[1]
    width = heads_per_step * DH
    return pl.pallas_call(
        tail_kernel,
        grid=(H // heads_per_step,),
        in_specs=[
            pl.BlockSpec((heads_per_step, DH, DH), lambda i: (i, 0, 0)),
            pl.BlockSpec((heads_per_step, rows, DH), lambda i: (i, 0, 0)),
            pl.BlockSpec((heads_per_step, rows, DH), lambda i: (i, 0, 0)),
            pl.BlockSpec((1, width), lambda i: (0, i)),
        ],
        out_specs=pl.BlockSpec((rows, width), lambda i: (0, i)),
        out_shape=jax.ShapeDtypeStruct((rows, H * DH), jnp.bfloat16),
    )(memory, queries, within, gains)


def tail_gathered_kernel(here_ref, g_ref, p_ref, q_ref, w_ref, gain_ref, o_ref):
    here = here_ref[0]
    for j in range(p_ref.shape[0]):
        state = p_ref[j]
        for c in range(g_ref.shape[0]):
            state = state + jnp.where(c < here, g_ref[c, j].astype(jnp.float32), 0.0)
        carried = jnp.dot(q_ref[j], state.astype(jnp.bfloat16), preferred_element_type=jnp.float32)
        numerator = carried + w_ref[j]
        scale = lax.rsqrt(jnp.mean(numerator * numerator, axis=-1, keepdims=True) + epsilon)
        part = slice(j * DH, (j + 1) * DH)
        o_ref[:, part] = (numerator * scale * gain_ref[:, part]).astype(o_ref.dtype)


def tail_from_memory_kernel(m_ref, q_ref, w_ref, gain_ref, prior_ref, o_ref):
    del prior_ref
    tail_kernel(m_ref, q_ref, w_ref, gain_ref, o_ref)


def attend_tail_split(here, gathered, prefix, late_memory, queries, within, gains, heads_per_step=4):
    rows = queries.shape[1]
    width = heads_per_step * DH
    n_piece = gathered.shape[0]
    early = gathered.shape[1] // heads_per_step
    late = late_memory.shape[0] // heads_per_step
    grid_spec = pltpu.PrefetchScalarGridSpec(
        num_scalar_prefetch=1,
        grid=(early,),
        in_specs=[
            pl.BlockSpec((n_piece, heads_per_step, DH, DH), lambda i, s: (0, i, 0, 0)),
            pl.BlockSpec((heads_per_step, DH, DH), lambda i, s: (i, 0, 0)),
            pl.BlockSpec((heads_per_step, rows, DH), lambda i, s: (i, 0, 0)),
            pl.BlockSpec((heads_per_step, rows, DH), lambda i, s: (i, 0, 0)),
            pl.BlockSpec((1, width), lambda i, s: (0, i)),
        ],
        out_specs=pl.BlockSpec((rows, width), lambda i, s: (0, i)),
    )
    first = pl.pallas_call(
        tail_gathered_kernel,
        grid_spec=grid_spec,
        out_shape=jax.ShapeDtypeStruct((rows, H * DH), jnp.bfloat16),
    )(here, gathered, prefix, queries, within, gains)
    return pl.pallas_call(
        tail_from_memory_kernel,
        grid=(late,),
        in_specs=[
            pl.BlockSpec((heads_per_step, DH, DH), lambda i: (i, 0, 0)),
            pl.BlockSpec((heads_per_step, rows, DH), lambda i: (early + i, 0, 0)),
            pl.BlockSpec((heads_per_step, rows, DH), lambda i: (early + i, 0, 0)),
            pl.BlockSpec((1, width), lambda i: (0, early + i)),
            pl.BlockSpec(memory_space=pl.ANY),
        ],
        out_specs=pl.BlockSpec((rows, width), lambda i: (0, early + i)),
        out_shape=jax.ShapeDtypeStruct((rows, H * DH), jnp.bfloat16),
        input_output_aliases={4: 0},
    )(late_memory, queries, within, gains, first)


def ring_shift(value, axis, shift, size, wrap=True):
    pairs = [(j, (j + shift) % size) for j in range(size) if wrap or j + shift < size]
    return lax.ppermute(value, axis, pairs)


def memory_before(local, filler):
    n_x = lax.axis_size("x")
    n_y = lax.axis_size("y")
    x_here = lax.axis_index("x")
    half = local.shape[0] // 2
    from_left = ring_shift(local, "x", 1, n_x)
    from_right = ring_shift(local, "x", -1, n_x)
    far = jnp.concatenate(
        [ring_shift(from_left[:half], "x", 1, n_x), ring_shift(from_right[half:], "x", -1, n_x)], axis=0
    )
    f32 = lambda v: v.astype(jnp.float32)
    row_total = f32(local) + f32(from_left) + f32(far) + f32(from_right)
    row_before = (
        jnp.where(x_here >= 1, f32(from_left), 0.0)
        + jnp.where(x_here >= 2, f32(far), 0.0)
        + jnp.where(x_here >= 3, f32(from_right), 0.0)
    )
    per = local.shape[0] // n_x
    quarter = lax.dynamic_slice_in_dim(row_total, x_here * per, per, axis=0)
    quarter, filler = lax.optimization_barrier((quarter, filler))
    rows_before = quarter * 0.0
    for shift in range(1, n_y):
        rows_before = rows_before + ring_shift(quarter, "y", shift, n_y, wrap=False)
    got = [rows_before] + [ring_shift(rows_before, "x", k, n_x) for k in range(1, n_x)]
    stacked = jnp.stack(got)
    order = (x_here - jnp.arange(n_x)) % n_x
    earlier_rows = jnp.take(stacked, order, axis=0).reshape(local.shape)
    return earlier_rows + row_before, filler


def body(tokens, input_gain, qkv_weight, head_gain, prefix_state):
    inputs = tokens[0].astype(jnp.float32)
    normed = inputs * lax.rsqrt(jnp.mean(inputs * inputs, axis=-1, keepdims=True) + epsilon)
    normed = (normed * input_gain.astype(jnp.float32)).astype(jnp.bfloat16)
    tok_rows = normed.shape[0]
    weight = lax.all_gather(qkv_weight, ("dp", "y", "x"), axis=1, tiled=True)
    half = H // 2
    k_early, v_early, local_early = kv_memory(normed, weight.T, 0, half)
    gathered = lax.all_gather(local_early[None], ("y", "x"), axis=0, tiled=True)
    k_late, v_late, local_late = kv_memory(normed, weight.T, half, H - half)
    key_feats = jnp.concatenate([k_early, k_late], axis=1).reshape(tok_rows, H, DH)
    values = jnp.concatenate([v_early, v_late], axis=1).reshape(tok_rows, H, DH)
    queries = jnp.dot(normed, weight[:, :D], preferred_element_type=jnp.float32)
    queries = feature_map(queries).astype(jnp.bfloat16)

    causal = jnp.arange(tok_rows)[:, None] >= jnp.arange(tok_rows)[None, :]
    scores = jnp.einsum(
        "bhd,chd->hbc", queries.reshape(tok_rows, H, DH), key_feats, preferred_element_type=jnp.float32
    )
    scores = jnp.where(causal[None], scores, 0.0).astype(jnp.bfloat16)
    within = jnp.einsum("hbc,che->hbe", scores, values, preferred_element_type=jnp.float32)
    before_late, within = memory_before(local_late, within)
    seq_here = lax.axis_index(("y", "x")).astype(jnp.int32).reshape(1)
    late_memory = prefix_state[0, half:] + before_late
    gains = head_gain.astype(jnp.float32).reshape(1, H * DH)
    attended = attend_tail_split(
        seq_here, gathered, prefix_state[0], late_memory,
        jnp.transpose(queries.reshape(tok_rows, H, DH), (1, 0, 2)), within, gains,
    )
    return attended.reshape(1, tok_rows, H * DH)


def solution(mesh):
    n_dp, n_seq = mesh.devices.shape
    n_x = int(round(n_seq ** 0.5))
    split = Mesh(mesh.devices.reshape(n_dp, n_seq // n_x, n_x), ("dp", "y", "x"))
    cols = ("y", "x")
    placed = (P("dp", cols, None), P(), P(None, ("dp", "y", "x")), P(), P("dp", None, None, None))
    return jax.shard_map(
        body, mesh=split, in_specs=placed, out_specs=P("dp", cols, None), check_vma=False
    )
```

```python
import jax
import jax.numpy as jnp
from jax import lax
from jax.experimental import pallas as pl
from jax.experimental.pallas import tpu as pltpu
from jax.sharding import Mesh, PartitionSpec as P

D = 2048
H = 16
DH = 128
BLOCK = 512


epsilon = 1e-05


def feature_map(inputs):
    return jnp.where(inputs > 0, inputs + 1.0, jnp.exp(jnp.minimum(inputs, 0.0)))


def kv_memory_kernel(x_ref, wk_ref, wv_ref, k_ref, v_ref, m_ref):
    x = x_ref[...]
    dims = (((1,), (1,)), ((), ()))
    k = lax.dot_general(x, wk_ref[...], dims, preferred_element_type=jnp.float32)
    k = feature_map(k).astype(jnp.bfloat16)
    v = lax.dot_general(x, wv_ref[...], dims, preferred_element_type=jnp.float32).astype(jnp.bfloat16)
    k_ref[...] = k
    v_ref[...] = v
    for j in range(m_ref.shape[0]):
        part = slice(j * DH, (j + 1) * DH)
        m = lax.dot_general(k[:, part], v[:, part], (((0,), (0,)), ((), ())), preferred_element_type=jnp.float32)
        m_ref[j] = m.astype(jnp.bfloat16)


def kv_memory(normed, weight_t, first_head, n_heads, heads_per_step=4):
    rows = normed.shape[0]
    width = heads_per_step * DH
    k_off = (D + first_head * DH) // width
    v_off = (2 * D + first_head * DH) // width
    return pl.pallas_call(
        kv_memory_kernel,
        grid=(n_heads // heads_per_step,),
        in_specs=[
            pl.BlockSpec((rows, D), lambda i: (0, 0)),
            pl.BlockSpec((width, D), lambda i: (k_off + i, 0)),
            pl.BlockSpec((width, D), lambda i: (v_off + i, 0)),
        ],
        out_specs=[
            pl.BlockSpec((rows, width), lambda i: (0, i)),
            pl.BlockSpec((rows, width), lambda i: (0, i)),
            pl.BlockSpec((heads_per_step, DH, DH), lambda i: (i, 0, 0)),
        ],
        out_shape=[
            jax.ShapeDtypeStruct((rows, n_heads * DH), jnp.bfloat16),
            jax.ShapeDtypeStruct((rows, n_heads * DH), jnp.bfloat16),
            jax.ShapeDtypeStruct((n_heads, DH, DH), jnp.bfloat16),
        ],
    )(normed, weight_t, weight_t)


def tail_kernel(m_ref, q_ref, w_ref, gain_ref, o_ref):
    for j in range(m_ref.shape[0]):
        carried = jnp.dot(q_ref[j], m_ref[j].astype(jnp.bfloat16), preferred_element_type=jnp.float32)
        numerator = carried + w_ref[j]
        scale = lax.rsqrt(jnp.mean(numerator * numerator, axis=-1, keepdims=True) + epsilon)
        part = slice(j * DH, (j + 1) * DH)
        o_ref[:, part] = (numerator * scale * gain_ref[:, part]).astype(o_ref.dtype)


def attend_tail(memory, queries, within, gains, heads_per_step=4):
    rows = queries.shape[1]
    width = heads_per_step * DH
    return pl.pallas_call(
        tail_kernel,
        grid=(H // heads_per_step,),
        in_specs=[
            pl.BlockSpec((heads_per_step, DH, DH), lambda i: (i, 0, 0)),
            pl.BlockSpec((heads_per_step, rows, DH), lambda i: (i, 0, 0)),
            pl.BlockSpec((heads_per_step, rows, DH), lambda i: (i, 0, 0)),
            pl.BlockSpec((1, width), lambda i: (0, i)),
        ],
        out_specs=pl.BlockSpec((rows, width), lambda i: (0, i)),
        out_shape=jax.ShapeDtypeStruct((rows, H * DH), jnp.bfloat16),
    )(memory, queries, within, gains)


def tail_gathered_kernel(here_ref, g_ref, p_ref, q_ref, w_ref, gain_ref, o_ref):
    here = here_ref[0]
    for j in range(p_ref.shape[0]):
        state = p_ref[j]
        for c in range(g_ref.shape[0]):
            state = state + jnp.where(c < here, g_ref[c, j].astype(jnp.float32), 0.0)
        carried = jnp.dot(q_ref[j], state.astype(jnp.bfloat16), preferred_element_type=jnp.float32)
        numerator = carried + w_ref[j]
        scale = lax.rsqrt(jnp.mean(numerator * numerator, axis=-1, keepdims=True) + epsilon)
        part = slice(j * DH, (j + 1) * DH)
        o_ref[:, part] = (numerator * scale * gain_ref[:, part]).astype(o_ref.dtype)


def tail_gathered_after_kernel(here_ref, g_ref, p_ref, q_ref, w_ref, gain_ref, prior_ref, o_ref):
    del prior_ref
    tail_gathered_kernel(here_ref, g_ref, p_ref, q_ref, w_ref, gain_ref, o_ref)


def attend_tail_split(here, gathered, prefix, late_memory, queries, within, gains, heads_per_step=4):
    rows = queries.shape[1]
    width = heads_per_step * DH
    n_piece = gathered.shape[0]
    early = gathered.shape[1] // heads_per_step
    late = late_memory.shape[0] // heads_per_step
    grid_spec = pltpu.PrefetchScalarGridSpec(
        num_scalar_prefetch=1,
        grid=(early,),
        in_specs=[
            pl.BlockSpec((n_piece, heads_per_step, DH, DH), lambda i, s: (0, i, 0, 0)),
            pl.BlockSpec((heads_per_step, DH, DH), lambda i, s: (i, 0, 0)),
            pl.BlockSpec((heads_per_step, rows, DH), lambda i, s: (i, 0, 0)),
            pl.BlockSpec((heads_per_step, rows, DH), lambda i, s: (i, 0, 0)),
            pl.BlockSpec((1, width), lambda i, s: (0, i)),
        ],
        out_specs=pl.BlockSpec((rows, width), lambda i, s: (0, i)),
    )
    first = pl.pallas_call(
        tail_kernel,
        grid=(late,),
        in_specs=[
            pl.BlockSpec((heads_per_step, DH, DH), lambda i: (i, 0, 0)),
            pl.BlockSpec((heads_per_step, rows, DH), lambda i: (early + i, 0, 0)),
            pl.BlockSpec((heads_per_step, rows, DH), lambda i: (early + i, 0, 0)),
            pl.BlockSpec((1, width), lambda i: (0, early + i)),
        ],
        out_specs=pl.BlockSpec((rows, width), lambda i: (0, early + i)),
        out_shape=jax.ShapeDtypeStruct((rows, H * DH), jnp.bfloat16),
    )(late_memory, queries, within, gains)
    grid_spec = pltpu.PrefetchScalarGridSpec(
        num_scalar_prefetch=1,
        grid=(early,),
        in_specs=[
            pl.BlockSpec((n_piece, heads_per_step, DH, DH), lambda i, s: (0, i, 0, 0)),
            pl.BlockSpec((heads_per_step, DH, DH), lambda i, s: (i, 0, 0)),
            pl.BlockSpec((heads_per_step, rows, DH), lambda i, s: (i, 0, 0)),
            pl.BlockSpec((heads_per_step, rows, DH), lambda i, s: (i, 0, 0)),
            pl.BlockSpec((1, width), lambda i, s: (0, i)),
            pl.BlockSpec(memory_space=pl.ANY),
        ],
        out_specs=pl.BlockSpec((rows, width), lambda i, s: (0, i)),
    )
    return pl.pallas_call(
        tail_gathered_after_kernel,
        grid_spec=grid_spec,
        out_shape=jax.ShapeDtypeStruct((rows, H * DH), jnp.bfloat16),
        input_output_aliases={6: 0},
    )(here, gathered, prefix, queries, within, gains, first)


def ring_shift(value, axis, shift, size, wrap=True):
    pairs = [(j, (j + shift) % size) for j in range(size) if wrap or j + shift < size]
    return lax.ppermute(value, axis, pairs)


def memory_before(local, filler):
    n_x = lax.axis_size("x")
    n_y = lax.axis_size("y")
    x_here = lax.axis_index("x")
    half = local.shape[0] // 2
    from_left = ring_shift(local, "x", 1, n_x)
    from_right = ring_shift(local, "x", -1, n_x)
    far = jnp.concatenate(
        [ring_shift(from_left[:half], "x", 1, n_x), ring_shift(from_right[half:], "x", -1, n_x)], axis=0
    )
    f32 = lambda v: v.astype(jnp.float32)
    row_total = f32(local) + f32(from_left) + f32(far) + f32(from_right)
    row_before = (
        jnp.where(x_here >= 1, f32(from_left), 0.0)
        + jnp.where(x_here >= 2, f32(far), 0.0)
        + jnp.where(x_here >= 3, f32(from_right), 0.0)
    )
    per = local.shape[0] // n_x
    quarter = lax.dynamic_slice_in_dim(row_total, x_here * per, per, axis=0)
    quarter, filler = lax.optimization_barrier((quarter, filler))
    rows_before = quarter * 0.0
    for shift in range(1, n_y):
        rows_before = rows_before + ring_shift(quarter, "y", shift, n_y, wrap=False)
    got = [rows_before] + [ring_shift(rows_before, "x", k, n_x) for k in range(1, n_x)]
    stacked = jnp.stack(got)
    order = (x_here - jnp.arange(n_x)) % n_x
    earlier_rows = jnp.take(stacked, order, axis=0).reshape(local.shape)
    return earlier_rows + row_before, filler


def body(tokens, input_gain, qkv_weight, head_gain, prefix_state):
    inputs = tokens[0].astype(jnp.float32)
    normed = inputs * lax.rsqrt(jnp.mean(inputs * inputs, axis=-1, keepdims=True) + epsilon)
    normed = (normed * input_gain.astype(jnp.float32)).astype(jnp.bfloat16)
    tok_rows = normed.shape[0]
    weight = lax.all_gather(qkv_weight, ("dp", "y", "x"), axis=1, tiled=True)
    half = H // 2
    k_early, v_early, local_early = kv_memory(normed, weight.T, 0, half)
    gathered = lax.all_gather(local_early[None], ("y", "x"), axis=0, tiled=True)
    k_late, v_late, local_late = kv_memory(normed, weight.T, half, H - half)
    key_feats = jnp.concatenate([k_early, k_late], axis=1).reshape(tok_rows, H, DH)
    values = jnp.concatenate([v_early, v_late], axis=1).reshape(tok_rows, H, DH)
    queries = jnp.dot(normed, weight[:, :D], preferred_element_type=jnp.float32)
    queries = feature_map(queries).astype(jnp.bfloat16)

    causal = jnp.arange(tok_rows)[:, None] >= jnp.arange(tok_rows)[None, :]
    scores = jnp.einsum(
        "bhd,chd->hbc", queries.reshape(tok_rows, H, DH), key_feats, preferred_element_type=jnp.float32
    )
    scores = jnp.where(causal[None], scores, 0.0).astype(jnp.bfloat16)
    within = jnp.einsum("hbc,che->hbe", scores, values, preferred_element_type=jnp.float32)
    before_late, within = memory_before(local_late, within)
    seq_here = lax.axis_index(("y", "x")).astype(jnp.int32).reshape(1)
    late_memory = prefix_state[0, half:] + before_late
    gains = head_gain.astype(jnp.float32).reshape(1, H * DH)
    attended = attend_tail_split(
        seq_here, gathered, prefix_state[0], late_memory,
        jnp.transpose(queries.reshape(tok_rows, H, DH), (1, 0, 2)), within, gains,
    )
    return attended.reshape(1, tok_rows, H * DH)


def solution(mesh):
    n_dp, n_seq = mesh.devices.shape
    n_x = int(round(n_seq ** 0.5))
    split = Mesh(mesh.devices.reshape(n_dp, n_seq // n_x, n_x), ("dp", "y", "x"))
    cols = ("y", "x")
    placed = (P("dp", cols, None), P(), P(None, ("dp", "y", "x")), P(), P("dp", None, None, None))
    return jax.shard_map(
        body, mesh=split, in_specs=placed, out_specs=P("dp", cols, None), check_vma=False
    )
```

```python
import jax
import jax.numpy as jnp
from jax import lax
from jax.experimental import pallas as pl
from jax.experimental.pallas import tpu as pltpu
from jax.sharding import Mesh, PartitionSpec as P

D = 2048
H = 16
DH = 128
BLOCK = 512


epsilon = 1e-05


def feature_map(inputs):
    return jnp.where(inputs > 0, inputs + 1.0, jnp.exp(jnp.minimum(inputs, 0.0)))


def kv_memory_kernel(x_ref, wk_ref, wv_ref, k_ref, v_ref, m_ref):
    x = x_ref[...]
    dims = (((1,), (1,)), ((), ()))
    k = lax.dot_general(x, wk_ref[...], dims, preferred_element_type=jnp.float32)
    k = feature_map(k).astype(jnp.bfloat16)
    v = lax.dot_general(x, wv_ref[...], dims, preferred_element_type=jnp.float32).astype(jnp.bfloat16)
    k_ref[...] = k
    v_ref[...] = v
    for j in range(m_ref.shape[0]):
        part = slice(j * DH, (j + 1) * DH)
        m = lax.dot_general(k[:, part], v[:, part], (((0,), (0,)), ((), ())), preferred_element_type=jnp.float32)
        m_ref[j] = m.astype(jnp.bfloat16)


def kv_memory(normed, weight_t, first_head, n_heads, heads_per_step=4):
    rows = normed.shape[0]
    width = heads_per_step * DH
    k_off = (D + first_head * DH) // width
    v_off = (2 * D + first_head * DH) // width
    return pl.pallas_call(
        kv_memory_kernel,
        grid=(n_heads // heads_per_step,),
        in_specs=[
            pl.BlockSpec((rows, D), lambda i: (0, 0)),
            pl.BlockSpec((width, D), lambda i: (k_off + i, 0)),
            pl.BlockSpec((width, D), lambda i: (v_off + i, 0)),
        ],
        out_specs=[
            pl.BlockSpec((rows, width), lambda i: (0, i)),
            pl.BlockSpec((rows, width), lambda i: (0, i)),
            pl.BlockSpec((heads_per_step, DH, DH), lambda i: (i, 0, 0)),
        ],
        out_shape=[
            jax.ShapeDtypeStruct((rows, n_heads * DH), jnp.bfloat16),
            jax.ShapeDtypeStruct((rows, n_heads * DH), jnp.bfloat16),
            jax.ShapeDtypeStruct((n_heads, DH, DH), jnp.bfloat16),
        ],
    )(normed, weight_t, weight_t)


def tail_kernel(m_ref, q_ref, w_ref, gain_ref, o_ref):
    for j in range(m_ref.shape[0]):
        carried = jnp.dot(q_ref[j], m_ref[j].astype(jnp.bfloat16), preferred_element_type=jnp.float32)
        numerator = carried + w_ref[j]
        scale = lax.rsqrt(jnp.mean(numerator * numerator, axis=-1, keepdims=True) + epsilon)
        part = slice(j * DH, (j + 1) * DH)
        o_ref[:, part] = (numerator * scale * gain_ref[:, part]).astype(o_ref.dtype)


def attend_tail(memory, queries, within, gains, heads_per_step=4):
    rows = queries.shape[1]
    width = heads_per_step * DH
    return pl.pallas_call(
        tail_kernel,
        grid=(H // heads_per_step,),
        in_specs=[
            pl.BlockSpec((heads_per_step, DH, DH), lambda i: (i, 0, 0)),
            pl.BlockSpec((heads_per_step, rows, DH), lambda i: (i, 0, 0)),
            pl.BlockSpec((heads_per_step, rows, DH), lambda i: (i, 0, 0)),
            pl.BlockSpec((1, width), lambda i: (0, i)),
        ],
        out_specs=pl.BlockSpec((rows, width), lambda i: (0, i)),
        out_shape=jax.ShapeDtypeStruct((rows, H * DH), jnp.bfloat16),
    )(memory, queries, within, gains)


def tail_gathered_kernel(here_ref, g_ref, p_ref, q_ref, w_ref, gain_ref, o_ref):
    here = here_ref[0]
    for j in range(p_ref.shape[0]):
        state = p_ref[j]
        for c in range(g_ref.shape[0]):
            state = state + jnp.where(c < here, g_ref[c, j].astype(jnp.float32), 0.0)
        carried = jnp.dot(q_ref[j], state.astype(jnp.bfloat16), preferred_element_type=jnp.float32)
        numerator = carried + w_ref[j]
        scale = lax.rsqrt(jnp.mean(numerator * numerator, axis=-1, keepdims=True) + epsilon)
        part = slice(j * DH, (j + 1) * DH)
        o_ref[:, part] = (numerator * scale * gain_ref[:, part]).astype(o_ref.dtype)


def tail_gathered_after_kernel(here_ref, g_ref, p_ref, q_ref, w_ref, gain_ref, prior_ref, o_ref):
    del prior_ref
    tail_gathered_kernel(here_ref, g_ref, p_ref, q_ref, w_ref, gain_ref, o_ref)


def attend_tail_split(here, gathered, prefix, late_memory, queries, within, gains, heads_per_step=4):
    rows = queries.shape[1]
    width = heads_per_step * DH
    n_piece = gathered.shape[0]
    early = gathered.shape[1] // heads_per_step
    late = late_memory.shape[0] // heads_per_step
    grid_spec = pltpu.PrefetchScalarGridSpec(
        num_scalar_prefetch=1,
        grid=(early,),
        in_specs=[
            pl.BlockSpec((n_piece, heads_per_step, DH, DH), lambda i, s: (0, i, 0, 0)),
            pl.BlockSpec((heads_per_step, DH, DH), lambda i, s: (i, 0, 0)),
            pl.BlockSpec((heads_per_step, rows, DH), lambda i, s: (i, 0, 0)),
            pl.BlockSpec((heads_per_step, rows, DH), lambda i, s: (i, 0, 0)),
            pl.BlockSpec((1, width), lambda i, s: (0, i)),
        ],
        out_specs=pl.BlockSpec((rows, width), lambda i, s: (0, i)),
    )
    first = pl.pallas_call(
        tail_kernel,
        grid=(late,),
        in_specs=[
            pl.BlockSpec((heads_per_step, DH, DH), lambda i: (i, 0, 0)),
            pl.BlockSpec((heads_per_step, rows, DH), lambda i: (early + i, 0, 0)),
            pl.BlockSpec((heads_per_step, rows, DH), lambda i: (early + i, 0, 0)),
            pl.BlockSpec((1, width), lambda i: (0, early + i)),
        ],
        out_specs=pl.BlockSpec((rows, width), lambda i: (0, early + i)),
        out_shape=jax.ShapeDtypeStruct((rows, H * DH), jnp.bfloat16),
    )(late_memory, queries, within, gains)
    grid_spec = pltpu.PrefetchScalarGridSpec(
        num_scalar_prefetch=1,
        grid=(early,),
        in_specs=[
            pl.BlockSpec((n_piece, heads_per_step, DH, DH), lambda i, s: (0, i, 0, 0)),
            pl.BlockSpec((heads_per_step, DH, DH), lambda i, s: (i, 0, 0)),
            pl.BlockSpec((heads_per_step, rows, DH), lambda i, s: (i, 0, 0)),
            pl.BlockSpec((heads_per_step, rows, DH), lambda i, s: (i, 0, 0)),
            pl.BlockSpec((1, width), lambda i, s: (0, i)),
            pl.BlockSpec(memory_space=pl.ANY),
        ],
        out_specs=pl.BlockSpec((rows, width), lambda i, s: (0, i)),
    )
    return pl.pallas_call(
        tail_gathered_after_kernel,
        grid_spec=grid_spec,
        out_shape=jax.ShapeDtypeStruct((rows, H * DH), jnp.bfloat16),
        input_output_aliases={6: 0},
    )(here, gathered, prefix, queries, within, gains, first)


def ring_shift(value, axis, shift, size, wrap=True):
    pairs = [(j, (j + shift) % size) for j in range(size) if wrap or j + shift < size]
    return lax.ppermute(value, axis, pairs)


def memory_before(local, filler):
    n_x = lax.axis_size("x")
    n_y = lax.axis_size("y")
    x_here = lax.axis_index("x")
    half = local.shape[0] // 2
    from_left = ring_shift(local, "x", 1, n_x)
    from_right = ring_shift(local, "x", -1, n_x)
    far = ring_shift(local, "x", 2, n_x)
    f32 = lambda v: v.astype(jnp.float32)
    row_total = f32(local) + f32(from_left) + f32(far) + f32(from_right)
    row_before = (
        jnp.where(x_here >= 1, f32(from_left), 0.0)
        + jnp.where(x_here >= 2, f32(far), 0.0)
        + jnp.where(x_here >= 3, f32(from_right), 0.0)
    )
    per = local.shape[0] // n_x
    quarter = lax.dynamic_slice_in_dim(row_total, x_here * per, per, axis=0)
    quarter, filler = lax.optimization_barrier((quarter, filler))
    rows_before = quarter * 0.0
    for shift in range(1, n_y):
        rows_before = rows_before + ring_shift(quarter, "y", shift, n_y, wrap=False)
    got = [rows_before] + [ring_shift(rows_before, "x", k, n_x) for k in range(1, n_x)]
    stacked = jnp.stack(got)
    order = (x_here - jnp.arange(n_x)) % n_x
    earlier_rows = jnp.take(stacked, order, axis=0).reshape(local.shape)
    return earlier_rows + row_before, filler


def body(tokens, input_gain, qkv_weight, head_gain, prefix_state):
    inputs = tokens[0].astype(jnp.float32)
    normed = inputs * lax.rsqrt(jnp.mean(inputs * inputs, axis=-1, keepdims=True) + epsilon)
    normed = (normed * input_gain.astype(jnp.float32)).astype(jnp.bfloat16)
    tok_rows = normed.shape[0]
    weight = lax.all_gather(qkv_weight, ("dp", "y", "x"), axis=1, tiled=True)
    half = H // 2
    k_early, v_early, local_early = kv_memory(normed, weight.T, 0, half)
    gathered = lax.all_gather(local_early[None], ("y", "x"), axis=0, tiled=True)
    k_late, v_late, local_late = kv_memory(normed, weight.T, half, H - half)
    key_feats = jnp.concatenate([k_early, k_late], axis=1).reshape(tok_rows, H, DH)
    values = jnp.concatenate([v_early, v_late], axis=1).reshape(tok_rows, H, DH)
    queries = jnp.dot(normed, weight[:, :D], preferred_element_type=jnp.float32)
    queries = feature_map(queries).astype(jnp.bfloat16)
    before_late, queries = memory_before(local_late, queries)

    causal = jnp.arange(tok_rows)[:, None] >= jnp.arange(tok_rows)[None, :]
    scores = jnp.einsum(
        "bhd,chd->hbc", queries.reshape(tok_rows, H, DH), key_feats, preferred_element_type=jnp.float32
    )
    scores = jnp.where(causal[None], scores, 0.0).astype(jnp.bfloat16)
    within = jnp.einsum("hbc,che->hbe", scores, values, preferred_element_type=jnp.float32)

    seq_here = lax.axis_index(("y", "x")).astype(jnp.int32).reshape(1)
    late_memory = prefix_state[0, half:] + before_late
    gains = head_gain.astype(jnp.float32).reshape(1, H * DH)
    attended = attend_tail_split(
        seq_here, gathered, prefix_state[0], late_memory,
        jnp.transpose(queries.reshape(tok_rows, H, DH), (1, 0, 2)), within, gains,
    )
    return attended.reshape(1, tok_rows, H * DH)


def solution(mesh):
    n_dp, n_seq = mesh.devices.shape
    n_x = int(round(n_seq ** 0.5))
    split = Mesh(mesh.devices.reshape(n_dp, n_seq // n_x, n_x), ("dp", "y", "x"))
    cols = ("y", "x")
    placed = (P("dp", cols, None), P(), P(None, ("dp", "y", "x")), P(), P("dp", None, None, None))
    return jax.shard_map(
        body, mesh=split, in_specs=placed, out_specs=P("dp", cols, None), check_vma=False
    )
```

```python
import jax
import jax.numpy as jnp
from jax import lax
from jax.experimental import pallas as pl
from jax.experimental.pallas import tpu as pltpu
from jax.sharding import Mesh, PartitionSpec as P

D = 2048
H = 16
DH = 128
BLOCK = 512


epsilon = 1e-05


def feature_map(inputs):
    return jnp.where(inputs > 0, inputs + 1.0, jnp.exp(jnp.minimum(inputs, 0.0)))


def kv_memory_kernel(x_ref, wk_ref, wv_ref, k_ref, v_ref, m_ref):
    x = x_ref[...]
    dims = (((1,), (1,)), ((), ()))
    k = lax.dot_general(x, wk_ref[...], dims, preferred_element_type=jnp.float32)
    k = feature_map(k).astype(jnp.bfloat16)
    v = lax.dot_general(x, wv_ref[...], dims, preferred_element_type=jnp.float32).astype(jnp.bfloat16)
    k_ref[...] = k
    v_ref[...] = v
    for j in range(m_ref.shape[0]):
        part = slice(j * DH, (j + 1) * DH)
        m = lax.dot_general(k[:, part], v[:, part], (((0,), (0,)), ((), ())), preferred_element_type=jnp.float32)
        m_ref[j] = m.astype(jnp.bfloat16)


def kv_memory(normed, weight_t, first_head, n_heads, heads_per_step=4):
    rows = normed.shape[0]
    width = heads_per_step * DH
    k_off = (D + first_head * DH) // width
    v_off = (2 * D + first_head * DH) // width
    return pl.pallas_call(
        kv_memory_kernel,
        grid=(n_heads // heads_per_step,),
        in_specs=[
            pl.BlockSpec((rows, D), lambda i: (0, 0)),
            pl.BlockSpec((width, D), lambda i: (k_off + i, 0)),
            pl.BlockSpec((width, D), lambda i: (v_off + i, 0)),
        ],
        out_specs=[
            pl.BlockSpec((rows, width), lambda i: (0, i)),
            pl.BlockSpec((rows, width), lambda i: (0, i)),
            pl.BlockSpec((heads_per_step, DH, DH), lambda i: (i, 0, 0)),
        ],
        out_shape=[
            jax.ShapeDtypeStruct((rows, n_heads * DH), jnp.bfloat16),
            jax.ShapeDtypeStruct((rows, n_heads * DH), jnp.bfloat16),
            jax.ShapeDtypeStruct((n_heads, DH, DH), jnp.bfloat16),
        ],
    )(normed, weight_t, weight_t)


def tail_kernel(m_ref, q_ref, w_ref, gain_ref, o_ref):
    for j in range(m_ref.shape[0]):
        carried = jnp.dot(q_ref[j], m_ref[j].astype(jnp.bfloat16), preferred_element_type=jnp.float32)
        numerator = carried + w_ref[j]
        scale = lax.rsqrt(jnp.mean(numerator * numerator, axis=-1, keepdims=True) + epsilon)
        part = slice(j * DH, (j + 1) * DH)
        o_ref[:, part] = (numerator * scale * gain_ref[:, part]).astype(o_ref.dtype)


def attend_tail(memory, queries, within, gains, heads_per_step=4):
    rows = queries.shape[1]
    width = heads_per_step * DH
    return pl.pallas_call(
        tail_kernel,
        grid=(H // heads_per_step,),
        in_specs=[
            pl.BlockSpec((heads_per_step, DH, DH), lambda i: (i, 0, 0)),
            pl.BlockSpec((heads_per_step, rows, DH), lambda i: (i, 0, 0)),
            pl.BlockSpec((heads_per_step, rows, DH), lambda i: (i, 0, 0)),
            pl.BlockSpec((1, width), lambda i: (0, i)),
        ],
        out_specs=pl.BlockSpec((rows, width), lambda i: (0, i)),
        out_shape=jax.ShapeDtypeStruct((rows, H * DH), jnp.bfloat16),
    )(memory, queries, within, gains)


def tail_gathered_kernel(here_ref, g_ref, p_ref, q_ref, w_ref, gain_ref, o_ref):
    here = here_ref[0]
    for j in range(p_ref.shape[0]):
        state = p_ref[j]
        for c in range(g_ref.shape[0]):
            state = state + jnp.where(c < here, g_ref[c, j].astype(jnp.float32), 0.0)
        carried = jnp.dot(q_ref[j], state.astype(jnp.bfloat16), preferred_element_type=jnp.float32)
        numerator = carried + w_ref[j]
        scale = lax.rsqrt(jnp.mean(numerator * numerator, axis=-1, keepdims=True) + epsilon)
        part = slice(j * DH, (j + 1) * DH)
        o_ref[:, part] = (numerator * scale * gain_ref[:, part]).astype(o_ref.dtype)


def tail_gathered_after_kernel(here_ref, g_ref, p_ref, q_ref, w_ref, gain_ref, prior_ref, o_ref):
    del prior_ref
    tail_gathered_kernel(here_ref, g_ref, p_ref, q_ref, w_ref, gain_ref, o_ref)


def attend_tail_split(here, gathered, prefix, late_memory, queries, within, gains, heads_per_step=2):
    rows = queries.shape[1]
    width = heads_per_step * DH
    n_piece = gathered.shape[0]
    early = gathered.shape[1] // heads_per_step
    late = late_memory.shape[0] // heads_per_step
    grid_spec = pltpu.PrefetchScalarGridSpec(
        num_scalar_prefetch=1,
        grid=(early,),
        in_specs=[
            pl.BlockSpec((n_piece, heads_per_step, DH, DH), lambda i, s: (0, i, 0, 0)),
            pl.BlockSpec((heads_per_step, DH, DH), lambda i, s: (i, 0, 0)),
            pl.BlockSpec((heads_per_step, rows, DH), lambda i, s: (i, 0, 0)),
            pl.BlockSpec((heads_per_step, rows, DH), lambda i, s: (i, 0, 0)),
            pl.BlockSpec((1, width), lambda i, s: (0, i)),
        ],
        out_specs=pl.BlockSpec((rows, width), lambda i, s: (0, i)),
    )
    first = pl.pallas_call(
        tail_kernel,
        grid=(late,),
        in_specs=[
            pl.BlockSpec((heads_per_step, DH, DH), lambda i: (i, 0, 0)),
            pl.BlockSpec((heads_per_step, rows, DH), lambda i: (early + i, 0, 0)),
            pl.BlockSpec((heads_per_step, rows, DH), lambda i: (early + i, 0, 0)),
            pl.BlockSpec((1, width), lambda i: (0, early + i)),
        ],
        out_specs=pl.BlockSpec((rows, width), lambda i: (0, early + i)),
        out_shape=jax.ShapeDtypeStruct((rows, H * DH), jnp.bfloat16),
    )(late_memory, queries, within, gains)
    grid_spec = pltpu.PrefetchScalarGridSpec(
        num_scalar_prefetch=1,
        grid=(early,),
        in_specs=[
            pl.BlockSpec((n_piece, heads_per_step, DH, DH), lambda i, s: (0, i, 0, 0)),
            pl.BlockSpec((heads_per_step, DH, DH), lambda i, s: (i, 0, 0)),
            pl.BlockSpec((heads_per_step, rows, DH), lambda i, s: (i, 0, 0)),
            pl.BlockSpec((heads_per_step, rows, DH), lambda i, s: (i, 0, 0)),
            pl.BlockSpec((1, width), lambda i, s: (0, i)),
            pl.BlockSpec(memory_space=pl.ANY),
        ],
        out_specs=pl.BlockSpec((rows, width), lambda i, s: (0, i)),
    )
    return pl.pallas_call(
        tail_gathered_after_kernel,
        grid_spec=grid_spec,
        out_shape=jax.ShapeDtypeStruct((rows, H * DH), jnp.bfloat16),
        input_output_aliases={6: 0},
    )(here, gathered, prefix, queries, within, gains, first)


def ring_shift(value, axis, shift, size, wrap=True):
    pairs = [(j, (j + shift) % size) for j in range(size) if wrap or j + shift < size]
    return lax.ppermute(value, axis, pairs)


def memory_before(local, filler):
    n_x = lax.axis_size("x")
    n_y = lax.axis_size("y")
    x_here = lax.axis_index("x")
    half = local.shape[0] // 2
    from_left = ring_shift(local, "x", 1, n_x)
    from_right = ring_shift(local, "x", -1, n_x)
    far = ring_shift(local, "x", 2, n_x)
    f32 = lambda v: v.astype(jnp.float32)
    row_total = f32(local) + f32(from_left) + f32(far) + f32(from_right)
    row_before = (
        jnp.where(x_here >= 1, f32(from_left), 0.0)
        + jnp.where(x_here >= 2, f32(far), 0.0)
        + jnp.where(x_here >= 3, f32(from_right), 0.0)
    )
    per = local.shape[0] // n_x
    quarter = lax.dynamic_slice_in_dim(row_total, x_here * per, per, axis=0)
    quarter, filler = lax.optimization_barrier((quarter, filler))
    rows_before = quarter * 0.0
    for shift in range(1, n_y):
        rows_before = rows_before + ring_shift(quarter, "y", shift, n_y, wrap=False)
    got = [rows_before] + [ring_shift(rows_before, "x", k, n_x) for k in range(1, n_x)]
    stacked = jnp.stack(got)
    order = (x_here - jnp.arange(n_x)) % n_x
    earlier_rows = jnp.take(stacked, order, axis=0).reshape(local.shape)
    return earlier_rows + row_before, filler


def body(tokens, input_gain, qkv_weight, head_gain, prefix_state):
    inputs = tokens[0].astype(jnp.float32)
    normed = inputs * lax.rsqrt(jnp.mean(inputs * inputs, axis=-1, keepdims=True) + epsilon)
    normed = (normed * input_gain.astype(jnp.float32)).astype(jnp.bfloat16)
    tok_rows = normed.shape[0]
    weight = lax.all_gather(qkv_weight, ("dp", "y", "x"), axis=1, tiled=True)
    half = H // 2
    k_early, v_early, local_early = kv_memory(normed, weight.T, 0, half)
    gathered = lax.all_gather(local_early[None], ("y", "x"), axis=0, tiled=True)
    k_late, v_late, local_late = kv_memory(normed, weight.T, half, H - half)
    key_feats = jnp.concatenate([k_early, k_late], axis=1).reshape(tok_rows, H, DH)
    values = jnp.concatenate([v_early, v_late], axis=1).reshape(tok_rows, H, DH)
    queries = jnp.dot(normed, weight[:, :D], preferred_element_type=jnp.float32)
    queries = feature_map(queries).astype(jnp.bfloat16)
    before_late, queries = memory_before(local_late, queries)

    causal = jnp.arange(tok_rows)[:, None] >= jnp.arange(tok_rows)[None, :]
    scores = jnp.einsum(
        "bhd,chd->hbc", queries.reshape(tok_rows, H, DH), key_feats, preferred_element_type=jnp.float32
    )
    scores = jnp.where(causal[None], scores, 0.0).astype(jnp.bfloat16)
    within = jnp.einsum("hbc,che->hbe", scores, values, preferred_element_type=jnp.float32)

    seq_here = lax.axis_index(("y", "x")).astype(jnp.int32).reshape(1)
    late_memory = prefix_state[0, half:] + before_late
    gains = head_gain.astype(jnp.float32).reshape(1, H * DH)
    attended = attend_tail_split(
        seq_here, gathered, prefix_state[0], late_memory,
        jnp.transpose(queries.reshape(tok_rows, H, DH), (1, 0, 2)), within, gains,
    )
    return attended.reshape(1, tok_rows, H * DH)


def solution(mesh):
    n_dp, n_seq = mesh.devices.shape
    n_x = int(round(n_seq ** 0.5))
    split = Mesh(mesh.devices.reshape(n_dp, n_seq // n_x, n_x), ("dp", "y", "x"))
    cols = ("y", "x")
    placed = (P("dp", cols, None), P(), P(None, ("dp", "y", "x")), P(), P("dp", None, None, None))
    return jax.shard_map(
        body, mesh=split, in_specs=placed, out_specs=P("dp", cols, None), check_vma=False
    )
```

```python
import jax
import jax.numpy as jnp
from jax import lax
from jax.experimental import pallas as pl
from jax.experimental.pallas import tpu as pltpu
from jax.sharding import Mesh, PartitionSpec as P

D = 2048
H = 16
DH = 128
BLOCK = 512


epsilon = 1e-05


def feature_map(inputs):
    return jnp.where(inputs > 0, inputs + 1.0, jnp.exp(jnp.minimum(inputs, 0.0)))


def kv_memory_kernel(x_ref, wk_ref, wv_ref, k_ref, v_ref, m_ref):
    x = x_ref[...]
    dims = (((1,), (1,)), ((), ()))
    k = lax.dot_general(x, wk_ref[...], dims, preferred_element_type=jnp.float32)
    k = feature_map(k).astype(jnp.bfloat16)
    v = lax.dot_general(x, wv_ref[...], dims, preferred_element_type=jnp.float32).astype(jnp.bfloat16)
    k_ref[...] = k
    v_ref[...] = v
    for j in range(m_ref.shape[0]):
        part = slice(j * DH, (j + 1) * DH)
        m = lax.dot_general(k[:, part], v[:, part], (((0,), (0,)), ((), ())), preferred_element_type=jnp.float32)
        m_ref[j] = m.astype(jnp.bfloat16)


def kv_memory(normed, weight_t, first_head, n_heads, heads_per_step=4):
    rows = normed.shape[0]
    width = heads_per_step * DH
    k_off = (D + first_head * DH) // width
    v_off = (2 * D + first_head * DH) // width
    return pl.pallas_call(
        kv_memory_kernel,
        grid=(n_heads // heads_per_step,),
        in_specs=[
            pl.BlockSpec((rows, D), lambda i: (0, 0)),
            pl.BlockSpec((width, D), lambda i: (k_off + i, 0)),
            pl.BlockSpec((width, D), lambda i: (v_off + i, 0)),
        ],
        out_specs=[
            pl.BlockSpec((rows, width), lambda i: (0, i)),
            pl.BlockSpec((rows, width), lambda i: (0, i)),
            pl.BlockSpec((heads_per_step, DH, DH), lambda i: (i, 0, 0)),
        ],
        out_shape=[
            jax.ShapeDtypeStruct((rows, n_heads * DH), jnp.bfloat16),
            jax.ShapeDtypeStruct((rows, n_heads * DH), jnp.bfloat16),
            jax.ShapeDtypeStruct((n_heads, DH, DH), jnp.bfloat16),
        ],
    )(normed, weight_t, weight_t)


def tail_kernel(m_ref, q_ref, w_ref, gain_ref, o_ref):
    for j in range(m_ref.shape[0]):
        carried = jnp.dot(q_ref[j], m_ref[j].astype(jnp.bfloat16), preferred_element_type=jnp.float32)
        numerator = carried + w_ref[j]
        scale = lax.rsqrt(jnp.mean(numerator * numerator, axis=-1, keepdims=True) + epsilon)
        part = slice(j * DH, (j + 1) * DH)
        o_ref[:, part] = (numerator * scale * gain_ref[:, part]).astype(o_ref.dtype)


def attend_tail(memory, queries, within, gains, heads_per_step=4):
    rows = queries.shape[1]
    width = heads_per_step * DH
    return pl.pallas_call(
        tail_kernel,
        grid=(H // heads_per_step,),
        in_specs=[
            pl.BlockSpec((heads_per_step, DH, DH), lambda i: (i, 0, 0)),
            pl.BlockSpec((heads_per_step, rows, DH), lambda i: (i, 0, 0)),
            pl.BlockSpec((heads_per_step, rows, DH), lambda i: (i, 0, 0)),
            pl.BlockSpec((1, width), lambda i: (0, i)),
        ],
        out_specs=pl.BlockSpec((rows, width), lambda i: (0, i)),
        out_shape=jax.ShapeDtypeStruct((rows, H * DH), jnp.bfloat16),
    )(memory, queries, within, gains)


def tail_gathered_kernel(here_ref, g_ref, p_ref, q_ref, w_ref, gain_ref, o_ref):
    here = here_ref[0]
    for j in range(p_ref.shape[0]):
        state = p_ref[j]
        for c in range(g_ref.shape[0]):
            state = state + jnp.where(c < here, g_ref[c, j].astype(jnp.float32), 0.0)
        carried = jnp.dot(q_ref[j], state.astype(jnp.bfloat16), preferred_element_type=jnp.float32)
        numerator = carried + w_ref[j]
        scale = lax.rsqrt(jnp.mean(numerator * numerator, axis=-1, keepdims=True) + epsilon)
        part = slice(j * DH, (j + 1) * DH)
        o_ref[:, part] = (numerator * scale * gain_ref[:, part]).astype(o_ref.dtype)


def tail_gathered_after_kernel(here_ref, g_ref, p_ref, q_ref, w_ref, gain_ref, prior_ref, o_ref):
    del prior_ref
    tail_gathered_kernel(here_ref, g_ref, p_ref, q_ref, w_ref, gain_ref, o_ref)


def attend_tail_split(here, gathered, prefix, late_memory, queries, within, gains, heads_per_step=8):
    rows = queries.shape[1]
    width = heads_per_step * DH
    n_piece = gathered.shape[0]
    early = gathered.shape[1] // heads_per_step
    late = late_memory.shape[0] // heads_per_step
    grid_spec = pltpu.PrefetchScalarGridSpec(
        num_scalar_prefetch=1,
        grid=(early,),
        in_specs=[
            pl.BlockSpec((n_piece, heads_per_step, DH, DH), lambda i, s: (0, i, 0, 0)),
            pl.BlockSpec((heads_per_step, DH, DH), lambda i, s: (i, 0, 0)),
            pl.BlockSpec((heads_per_step, rows, DH), lambda i, s: (i, 0, 0)),
            pl.BlockSpec((heads_per_step, rows, DH), lambda i, s: (i, 0, 0)),
            pl.BlockSpec((1, width), lambda i, s: (0, i)),
        ],
        out_specs=pl.BlockSpec((rows, width), lambda i, s: (0, i)),
    )
    first = pl.pallas_call(
        tail_kernel,
        grid=(late,),
        in_specs=[
            pl.BlockSpec((heads_per_step, DH, DH), lambda i: (i, 0, 0)),
            pl.BlockSpec((heads_per_step, rows, DH), lambda i: (early + i, 0, 0)),
            pl.BlockSpec((heads_per_step, rows, DH), lambda i: (early + i, 0, 0)),
            pl.BlockSpec((1, width), lambda i: (0, early + i)),
        ],
        out_specs=pl.BlockSpec((rows, width), lambda i: (0, early + i)),
        out_shape=jax.ShapeDtypeStruct((rows, H * DH), jnp.bfloat16),
    )(late_memory, queries, within, gains)
    grid_spec = pltpu.PrefetchScalarGridSpec(
        num_scalar_prefetch=1,
        grid=(early,),
        in_specs=[
            pl.BlockSpec((n_piece, heads_per_step, DH, DH), lambda i, s: (0, i, 0, 0)),
            pl.BlockSpec((heads_per_step, DH, DH), lambda i, s: (i, 0, 0)),
            pl.BlockSpec((heads_per_step, rows, DH), lambda i, s: (i, 0, 0)),
            pl.BlockSpec((heads_per_step, rows, DH), lambda i, s: (i, 0, 0)),
            pl.BlockSpec((1, width), lambda i, s: (0, i)),
            pl.BlockSpec(memory_space=pl.ANY),
        ],
        out_specs=pl.BlockSpec((rows, width), lambda i, s: (0, i)),
    )
    return pl.pallas_call(
        tail_gathered_after_kernel,
        grid_spec=grid_spec,
        out_shape=jax.ShapeDtypeStruct((rows, H * DH), jnp.bfloat16),
        input_output_aliases={6: 0},
    )(here, gathered, prefix, queries, within, gains, first)


def ring_shift(value, axis, shift, size, wrap=True):
    pairs = [(j, (j + shift) % size) for j in range(size) if wrap or j + shift < size]
    return lax.ppermute(value, axis, pairs)


def memory_before(local, filler):
    n_x = lax.axis_size("x")
    n_y = lax.axis_size("y")
    x_here = lax.axis_index("x")
    half = local.shape[0] // 2
    from_left = ring_shift(local, "x", 1, n_x)
    from_right = ring_shift(local, "x", -1, n_x)
    far = ring_shift(local, "x", 2, n_x)
    f32 = lambda v: v.astype(jnp.float32)
    row_total = f32(local) + f32(from_left) + f32(far) + f32(from_right)
    row_before = (
        jnp.where(x_here >= 1, f32(from_left), 0.0)
        + jnp.where(x_here >= 2, f32(far), 0.0)
        + jnp.where(x_here >= 3, f32(from_right), 0.0)
    )
    per = local.shape[0] // n_x
    quarter = lax.dynamic_slice_in_dim(row_total, x_here * per, per, axis=0)
    quarter, filler = lax.optimization_barrier((quarter, filler))
    rows_before = quarter * 0.0
    for shift in range(1, n_y):
        rows_before = rows_before + ring_shift(quarter, "y", shift, n_y, wrap=False)
    got = [rows_before] + [ring_shift(rows_before, "x", k, n_x) for k in range(1, n_x)]
    stacked = jnp.stack(got)
    order = (x_here - jnp.arange(n_x)) % n_x
    earlier_rows = jnp.take(stacked, order, axis=0).reshape(local.shape)
    return earlier_rows + row_before, filler


def body(tokens, input_gain, qkv_weight, head_gain, prefix_state):
    inputs = tokens[0].astype(jnp.float32)
    normed = inputs * lax.rsqrt(jnp.mean(inputs * inputs, axis=-1, keepdims=True) + epsilon)
    normed = (normed * input_gain.astype(jnp.float32)).astype(jnp.bfloat16)
    tok_rows = normed.shape[0]
    weight = lax.all_gather(qkv_weight, ("dp", "y", "x"), axis=1, tiled=True)
    half = H // 2
    k_early, v_early, local_early = kv_memory(normed, weight.T, 0, half)
    gathered = lax.all_gather(local_early[None], ("y", "x"), axis=0, tiled=True)
    k_late, v_late, local_late = kv_memory(normed, weight.T, half, H - half)
    key_feats = jnp.concatenate([k_early, k_late], axis=1).reshape(tok_rows, H, DH)
    values = jnp.concatenate([v_early, v_late], axis=1).reshape(tok_rows, H, DH)
    queries = jnp.dot(normed, weight[:, :D], preferred_element_type=jnp.float32)
    queries = feature_map(queries).astype(jnp.bfloat16)
    before_late, queries = memory_before(local_late, queries)

    causal = jnp.arange(tok_rows)[:, None] >= jnp.arange(tok_rows)[None, :]
    scores = jnp.einsum(
        "bhd,chd->hbc", queries.reshape(tok_rows, H, DH), key_feats, preferred_element_type=jnp.float32
    )
    scores = jnp.where(causal[None], scores, 0.0).astype(jnp.bfloat16)
    within = jnp.einsum("hbc,che->hbe", scores, values, preferred_element_type=jnp.float32)

    seq_here = lax.axis_index(("y", "x")).astype(jnp.int32).reshape(1)
    late_memory = prefix_state[0, half:] + before_late
    gains = head_gain.astype(jnp.float32).reshape(1, H * DH)
    attended = attend_tail_split(
        seq_here, gathered, prefix_state[0], late_memory,
        jnp.transpose(queries.reshape(tok_rows, H, DH), (1, 0, 2)), within, gains,
    )
    return attended.reshape(1, tok_rows, H * DH)


def solution(mesh):
    n_dp, n_seq = mesh.devices.shape
    n_x = int(round(n_seq ** 0.5))
    split = Mesh(mesh.devices.reshape(n_dp, n_seq // n_x, n_x), ("dp", "y", "x"))
    cols = ("y", "x")
    placed = (P("dp", cols, None), P(), P(None, ("dp", "y", "x")), P(), P("dp", None, None, None))
    return jax.shard_map(
        body, mesh=split, in_specs=placed, out_specs=P("dp", cols, None), check_vma=False
    )
```

```python
import jax
import jax.numpy as jnp
from jax import lax
from jax.experimental import pallas as pl
from jax.experimental.pallas import tpu as pltpu
from jax.sharding import Mesh, PartitionSpec as P

D = 2048
H = 16
DH = 128
BLOCK = 512


epsilon = 1e-05


def feature_map(inputs):
    return jnp.where(inputs > 0, inputs + 1.0, jnp.exp(jnp.minimum(inputs, 0.0)))


def kv_memory_kernel(x_ref, wk_ref, wv_ref, k_ref, v_ref, m_ref):
    x = x_ref[...]
    dims = (((1,), (1,)), ((), ()))
    k = lax.dot_general(x, wk_ref[...], dims, preferred_element_type=jnp.float32)
    k = feature_map(k).astype(jnp.bfloat16)
    v = lax.dot_general(x, wv_ref[...], dims, preferred_element_type=jnp.float32).astype(jnp.bfloat16)
    k_ref[...] = k
    v_ref[...] = v
    for j in range(m_ref.shape[0]):
        part = slice(j * DH, (j + 1) * DH)
        m = lax.dot_general(k[:, part], v[:, part], (((0,), (0,)), ((), ())), preferred_element_type=jnp.float32)
        m_ref[j] = m.astype(jnp.bfloat16)


def kv_memory(normed, weight_t, first_head, n_heads, heads_per_step=8):
    rows = normed.shape[0]
    width = heads_per_step * DH
    k_off = (D + first_head * DH) // width
    v_off = (2 * D + first_head * DH) // width
    return pl.pallas_call(
        kv_memory_kernel,
        grid=(n_heads // heads_per_step,),
        in_specs=[
            pl.BlockSpec((rows, D), lambda i: (0, 0)),
            pl.BlockSpec((width, D), lambda i: (k_off + i, 0)),
            pl.BlockSpec((width, D), lambda i: (v_off + i, 0)),
        ],
        out_specs=[
            pl.BlockSpec((rows, width), lambda i: (0, i)),
            pl.BlockSpec((rows, width), lambda i: (0, i)),
            pl.BlockSpec((heads_per_step, DH, DH), lambda i: (i, 0, 0)),
        ],
        out_shape=[
            jax.ShapeDtypeStruct((rows, n_heads * DH), jnp.bfloat16),
            jax.ShapeDtypeStruct((rows, n_heads * DH), jnp.bfloat16),
            jax.ShapeDtypeStruct((n_heads, DH, DH), jnp.bfloat16),
        ],
    )(normed, weight_t, weight_t)


def tail_kernel(m_ref, q_ref, w_ref, gain_ref, o_ref):
    for j in range(m_ref.shape[0]):
        carried = jnp.dot(q_ref[j], m_ref[j].astype(jnp.bfloat16), preferred_element_type=jnp.float32)
        numerator = carried + w_ref[j]
        scale = lax.rsqrt(jnp.mean(numerator * numerator, axis=-1, keepdims=True) + epsilon)
        part = slice(j * DH, (j + 1) * DH)
        o_ref[:, part] = (numerator * scale * gain_ref[:, part]).astype(o_ref.dtype)


def attend_tail(memory, queries, within, gains, heads_per_step=4):
    rows = queries.shape[1]
    width = heads_per_step * DH
    return pl.pallas_call(
        tail_kernel,
        grid=(H // heads_per_step,),
        in_specs=[
            pl.BlockSpec((heads_per_step, DH, DH), lambda i: (i, 0, 0)),
            pl.BlockSpec((heads_per_step, rows, DH), lambda i: (i, 0, 0)),
            pl.BlockSpec((heads_per_step, rows, DH), lambda i: (i, 0, 0)),
            pl.BlockSpec((1, width), lambda i: (0, i)),
        ],
        out_specs=pl.BlockSpec((rows, width), lambda i: (0, i)),
        out_shape=jax.ShapeDtypeStruct((rows, H * DH), jnp.bfloat16),
    )(memory, queries, within, gains)


def tail_gathered_kernel(here_ref, g_ref, p_ref, q_ref, w_ref, gain_ref, o_ref):
    here = here_ref[0]
    for j in range(p_ref.shape[0]):
        state = p_ref[j]
        for c in range(g_ref.shape[0]):
            state = state + jnp.where(c < here, g_ref[c, j].astype(jnp.float32), 0.0)
        carried = jnp.dot(q_ref[j], state.astype(jnp.bfloat16), preferred_element_type=jnp.float32)
        numerator = carried + w_ref[j]
        scale = lax.rsqrt(jnp.mean(numerator * numerator, axis=-1, keepdims=True) + epsilon)
        part = slice(j * DH, (j + 1) * DH)
        o_ref[:, part] = (numerator * scale * gain_ref[:, part]).astype(o_ref.dtype)


def tail_gathered_after_kernel(here_ref, g_ref, p_ref, q_ref, w_ref, gain_ref, prior_ref, o_ref):
    del prior_ref
    tail_gathered_kernel(here_ref, g_ref, p_ref, q_ref, w_ref, gain_ref, o_ref)


def attend_tail_split(here, gathered, prefix, late_memory, queries, within, gains, heads_per_step=4):
    rows = queries.shape[1]
    width = heads_per_step * DH
    n_piece = gathered.shape[0]
    early = gathered.shape[1] // heads_per_step
    late = late_memory.shape[0] // heads_per_step
    grid_spec = pltpu.PrefetchScalarGridSpec(
        num_scalar_prefetch=1,
        grid=(early,),
        in_specs=[
            pl.BlockSpec((n_piece, heads_per_step, DH, DH), lambda i, s: (0, i, 0, 0)),
            pl.BlockSpec((heads_per_step, DH, DH), lambda i, s: (i, 0, 0)),
            pl.BlockSpec((heads_per_step, rows, DH), lambda i, s: (i, 0, 0)),
            pl.BlockSpec((heads_per_step, rows, DH), lambda i, s: (i, 0, 0)),
            pl.BlockSpec((1, width), lambda i, s: (0, i)),
        ],
        out_specs=pl.BlockSpec((rows, width), lambda i, s: (0, i)),
    )
    first = pl.pallas_call(
        tail_kernel,
        grid=(late,),
        in_specs=[
            pl.BlockSpec((heads_per_step, DH, DH), lambda i: (i, 0, 0)),
            pl.BlockSpec((heads_per_step, rows, DH), lambda i: (early + i, 0, 0)),
            pl.BlockSpec((heads_per_step, rows, DH), lambda i: (early + i, 0, 0)),
            pl.BlockSpec((1, width), lambda i: (0, early + i)),
        ],
        out_specs=pl.BlockSpec((rows, width), lambda i: (0, early + i)),
        out_shape=jax.ShapeDtypeStruct((rows, H * DH), jnp.bfloat16),
    )(late_memory, queries, within, gains)
    grid_spec = pltpu.PrefetchScalarGridSpec(
        num_scalar_prefetch=1,
        grid=(early,),
        in_specs=[
            pl.BlockSpec((n_piece, heads_per_step, DH, DH), lambda i, s: (0, i, 0, 0)),
            pl.BlockSpec((heads_per_step, DH, DH), lambda i, s: (i, 0, 0)),
            pl.BlockSpec((heads_per_step, rows, DH), lambda i, s: (i, 0, 0)),
            pl.BlockSpec((heads_per_step, rows, DH), lambda i, s: (i, 0, 0)),
            pl.BlockSpec((1, width), lambda i, s: (0, i)),
            pl.BlockSpec(memory_space=pl.ANY),
        ],
        out_specs=pl.BlockSpec((rows, width), lambda i, s: (0, i)),
    )
    return pl.pallas_call(
        tail_gathered_after_kernel,
        grid_spec=grid_spec,
        out_shape=jax.ShapeDtypeStruct((rows, H * DH), jnp.bfloat16),
        input_output_aliases={6: 0},
    )(here, gathered, prefix, queries, within, gains, first)


def ring_shift(value, axis, shift, size, wrap=True):
    pairs = [(j, (j + shift) % size) for j in range(size) if wrap or j + shift < size]
    return lax.ppermute(value, axis, pairs)


def memory_before(local, filler):
    n_x = lax.axis_size("x")
    n_y = lax.axis_size("y")
    x_here = lax.axis_index("x")
    half = local.shape[0] // 2
    from_left = ring_shift(local, "x", 1, n_x)
    from_right = ring_shift(local, "x", -1, n_x)
    far = ring_shift(local, "x", 2, n_x)
    f32 = lambda v: v.astype(jnp.float32)
    row_total = f32(local) + f32(from_left) + f32(far) + f32(from_right)
    row_before = (
        jnp.where(x_here >= 1, f32(from_left), 0.0)
        + jnp.where(x_here >= 2, f32(far), 0.0)
        + jnp.where(x_here >= 3, f32(from_right), 0.0)
    )
    per = local.shape[0] // n_x
    quarter = lax.dynamic_slice_in_dim(row_total, x_here * per, per, axis=0)
    quarter, filler = lax.optimization_barrier((quarter, filler))
    rows_before = quarter * 0.0
    for shift in range(1, n_y):
        rows_before = rows_before + ring_shift(quarter, "y", shift, n_y, wrap=False)
    got = [rows_before] + [ring_shift(rows_before, "x", k, n_x) for k in range(1, n_x)]
    stacked = jnp.stack(got)
    order = (x_here - jnp.arange(n_x)) % n_x
    earlier_rows = jnp.take(stacked, order, axis=0).reshape(local.shape)
    return earlier_rows + row_before, filler


def body(tokens, input_gain, qkv_weight, head_gain, prefix_state):
    inputs = tokens[0].astype(jnp.float32)
    normed = inputs * lax.rsqrt(jnp.mean(inputs * inputs, axis=-1, keepdims=True) + epsilon)
    normed = (normed * input_gain.astype(jnp.float32)).astype(jnp.bfloat16)
    tok_rows = normed.shape[0]
    weight = lax.all_gather(qkv_weight, ("dp", "y", "x"), axis=1, tiled=True)
    half = H // 2
    k_early, v_early, local_early = kv_memory(normed, weight.T, 0, half)
    gathered = lax.all_gather(local_early[None], ("y", "x"), axis=0, tiled=True)
    k_late, v_late, local_late = kv_memory(normed, weight.T, half, H - half)
    key_feats = jnp.concatenate([k_early, k_late], axis=1).reshape(tok_rows, H, DH)
    values = jnp.concatenate([v_early, v_late], axis=1).reshape(tok_rows, H, DH)
    queries = jnp.dot(normed, weight[:, :D], preferred_element_type=jnp.float32)
    queries = feature_map(queries).astype(jnp.bfloat16)
    before_late, queries = memory_before(local_late, queries)

    causal = jnp.arange(tok_rows)[:, None] >= jnp.arange(tok_rows)[None, :]
    scores = jnp.einsum(
        "bhd,chd->hbc", queries.reshape(tok_rows, H, DH), key_feats, preferred_element_type=jnp.float32
    )
    scores = jnp.where(causal[None], scores, 0.0).astype(jnp.bfloat16)
    within = jnp.einsum("hbc,che->hbe", scores, values, preferred_element_type=jnp.float32)

    seq_here = lax.axis_index(("y", "x")).astype(jnp.int32).reshape(1)
    late_memory = prefix_state[0, half:] + before_late
    gains = head_gain.astype(jnp.float32).reshape(1, H * DH)
    attended = attend_tail_split(
        seq_here, gathered, prefix_state[0], late_memory,
        jnp.transpose(queries.reshape(tok_rows, H, DH), (1, 0, 2)), within, gains,
    )
    return attended.reshape(1, tok_rows, H * DH)


def solution(mesh):
    n_dp, n_seq = mesh.devices.shape
    n_x = int(round(n_seq ** 0.5))
    split = Mesh(mesh.devices.reshape(n_dp, n_seq // n_x, n_x), ("dp", "y", "x"))
    cols = ("y", "x")
    placed = (P("dp", cols, None), P(), P(None, ("dp", "y", "x")), P(), P("dp", None, None, None))
    return jax.shard_map(
        body, mesh=split, in_specs=placed, out_specs=P("dp", cols, None), check_vma=False
    )
```
